512 devices in a mesh: dp: 32 (over y, z_lo, core), ctx: 16 (over x, z_hi).
Axes of the slice: x: 4, y: 4, z: 16 (z_hi: 4, z_lo: 4; z = z_hi * 4 + z_lo), core: 2. Of those that a mesh axis runs over, the one named last changes fastest.
Arguments:
- branch_in: bfloat16 [32, 2048, 2816], P('dp', 'ctx'), may hold values from -6 to 6
- cotangent: bfloat16 [32, 2048, 2816], P('dp', 'ctx'), may hold values from -6 to 6
- weight_a: bfloat16 [256, 2816], P('dp', 'ctx'), may hold values from -0.375 to 0.375
- weight_x: bfloat16 [256, 2816], P('dp', 'ctx'), may hold values from -0.375 to 0.375
- conv_weight: bfloat16 [4, 2816], P(None, 'ctx'), may hold values from -3 to 3
- conv_bias: bfloat16 [2816], P('ctx'), may hold values from -3 to 3
- bias_a: bfloat16 [2816], P('ctx'), may hold values from -4 to 4
- bias_x: bfloat16 [2816], P('ctx'), may hold values from -4 to 4
- rate: bfloat16 [2816], P('ctx'), may hold values from 0 to 0.016, as said below
Outputs:
- grad_input: bfloat16 [32, 2048, 2816], P('dp', 'ctx')
- grad_weight_a: float32 [256, 2816], P('dp', 'ctx')
- grad_rate: float32 [2816], replicated
The draws below stay inside these ranges and needn't reach their ends.
Inputs may be any that keep to these rules, and one draw needn't show every extreme that they name: `rate`: positive in every channel.
All inputs are finite; a program needn't handle non-finite values.
Results may differ from the reference program's by a relative error of at most 0.006.
Values may be sent and summed in bfloat16 or wider, within the bound.
No kernel may reach another device: no remote copies, remote signals or barrier semaphores. Data moves between devices by JAX's collectives and lax.ppermute only.
A program may use at most 128 MiB of HBM per device.

```python
import math
import jax
import jax.numpy as jnp
from jax import lax

HEADW = 256
KW = 4
R = 2816
SEQ = 2048
BATCH = 32


def draw_rate(key, part):
    pick_key, slow_key, fast_key = jax.random.split(key, 3)
    share = 0.5
    chooser = jax.random.uniform(pick_key, (R,), jnp.float32)
    slow_rates = jnp.exp(jax.random.uniform(slow_key, (R,), jnp.float32, math.log(0.05 / SEQ), math.log(0.5 / SEQ)))
    fast_rates = jnp.exp(jax.random.uniform(fast_key, (R,), jnp.float32, math.log(0.002), math.log(0.014)))
    return jnp.where(chooser < share, slow_rates, fast_rates).astype(jnp.bfloat16)


def steps_of(stream_key, shape, shards, smallest, top_value):
    factor_of, own = 1.0, jax.random.fold_in(stream_key, 6)
    for dim, parts in shards:
        draws = jnp.exp(jax.random.uniform(jax.random.fold_in(own, dim), (parts,), jnp.float32, smallest / len(shards), top_value / len(shards)))
        factor_of = factor_of * jnp.repeat(draws, shape[dim] // parts).reshape([-1 if axis == dim else 1 for axis in range(len(shape))])
    return factor_of


def gaussian(stream_key, dims, spread, bound, shards=(), dtype=jnp.bfloat16):
    values = spread * jax.random.normal(stream_key, dims, jnp.float32)
    if shards:
        values = values * steps_of(stream_key, dims, shards, -0.22, 0.18)
    return jnp.clip(values, -bound, bound).astype(dtype)


def setup_inputs(seed: int = 0) -> dict:
    seeds = jax.random.split(jax.random.key(seed), 10)
    return {
        "branch_in": gaussian(seeds[0], (BATCH, SEQ, R), 1.0, 6.0, ((0, 32), (1, 16))),
        "cotangent": gaussian(seeds[1], (BATCH, SEQ, R), 1.0, 6.0, ((0, 32), (1, 16))),
        "weight_a": gaussian(seeds[2], (HEADW, R), HEADW ** -0.5, 0.375, ((0, 32), (1, 16))),
        "weight_x": gaussian(seeds[3], (HEADW, R), HEADW ** -0.5, 0.375, ((0, 32), (1, 16))),
        "conv_weight": gaussian(seeds[4], (KW, R), KW ** -0.5, 3.0, ((1, 16),)),
        "conv_bias": gaussian(seeds[5], (R,), 0.5, 3.0, ((0, 16),)),
        "bias_a": gaussian(seeds[6], (R,), 1.0, 4.0, ((0, 16),)),
        "bias_x": gaussian(seeds[7], (R,), 1.0, 4.0, ((0, 16),)),
        "rate": draw_rate(jax.random.fold_in(seeds[9], 71), 0),
    }


floor_value = 2.5e-07

def mix_heads(values, weights):
    tokens = values.shape[0]
    head_width = weights.shape[0]
    head_count = weights.shape[1] // head_width
    left = values.astype(jnp.float32).reshape(tokens, head_count, head_width)
    right = weights.astype(jnp.float32).reshape(head_width, head_count, head_width)
    result = jnp.einsum('thk,khj->thj', left, right, precision=lax.Precision.HIGHEST)
    return result.reshape(tokens, head_count * head_width)

def back_heads(grads, weights):
    tokens = grads.shape[0]
    head_width = weights.shape[0]
    head_count = weights.shape[1] // head_width
    left = grads.astype(jnp.float32).reshape(tokens, head_count, head_width)
    right = weights.astype(jnp.float32).reshape(head_width, head_count, head_width)
    result = jnp.einsum('thj,khj->thk', left, right, precision=lax.Precision.HIGHEST)
    return result.reshape(tokens, head_count * head_width)

def grad_heads(values, grads, head_width):
    tokens = values.shape[0]
    head_count = values.shape[1] // head_width
    left = values.astype(jnp.float32).reshape(tokens, head_count, head_width)
    right = grads.astype(jnp.float32).reshape(tokens, head_count, head_width)
    result = jnp.einsum('thk,thj->khj', left, right, precision=lax.Precision.HIGHEST)
    return result.reshape(head_width, head_count * head_width)

def combine(earlier, later):
    return (earlier[0] * later[0], later[0] * earlier[1] + later[1])

def reference(branch_in, cotangent, weight_a, weight_x, conv_weight, conv_bias, bias_a, bias_x, rate):
    taps_f = conv_weight.astype(jnp.float32)
    cbias = conv_bias.astype(jnp.float32)
    abias = bias_a.astype(jnp.float32)
    xbias = bias_x.astype(jnp.float32)
    rates = rate.astype(jnp.float32)
    taps = taps_f.shape[0]
    width = taps_f.shape[1]
    head_width = weight_a.shape[0]

    def one_sequence(pair):
        seq_in, seq_grad = pair
        length = seq_in.shape[0]
        padded = jnp.concatenate([jnp.zeros((taps - 1, width), jnp.float32), seq_in.astype(jnp.float32)], 0)
        conv = cbias
        for tap in range(taps):
            conv = conv + taps_f[tap] * padded[tap:tap + length]
        conv_b = conv.astype(jnp.bfloat16)
        conv_f = conv_b.astype(jnp.float32)
        recur_gate = jax.nn.sigmoid(mix_heads(conv_b, weight_a) + abias)
        input_gate = jax.nn.sigmoid(mix_heads(conv_b, weight_x) + xbias)
        log_decay = -8.0 * recur_gate * rates
        decay = jnp.exp(log_decay)
        one_minus = -jnp.expm1(2.0 * log_decay)
        multiplier = jnp.sqrt(jnp.maximum(one_minus, floor_value))
        drive = multiplier * input_gate * conv_f
        _, hidden = lax.associative_scan(combine, (decay, drive), axis=0)
        previous = jnp.concatenate([jnp.zeros((1, width), jnp.float32), hidden[:-1]], 0)
        upstream = seq_grad.astype(jnp.float32)
        coefs = jnp.concatenate([decay[1:], jnp.ones((1, width), jnp.float32)], 0)
        _, back = lax.associative_scan(combine, (coefs, upstream), reverse=True, axis=0)
        slope = jnp.where(one_minus > floor_value, 0.5 / multiplier, 0.0)
        d_mult = back * input_gate * conv_f
        d_log = back * previous * decay - 2.0 * decay * decay * d_mult * slope
        d_recur = (d_log * (-8.0 * rates) * recur_gate * (1.0 - recur_gate)).astype(jnp.bfloat16)
        d_input = (back * multiplier * conv_f * input_gate * (1.0 - input_gate)).astype(jnp.bfloat16)
        d_conv = back * multiplier * input_gate + back_heads(d_recur, weight_a) + back_heads(d_input, weight_x)
        dpad = jnp.concatenate([d_conv, jnp.zeros((taps - 1, width), jnp.float32)], 0)
        grad_in = jnp.zeros((length, width), jnp.float32)
        for tap in range(taps):
            start = taps - 1 - tap
            grad_in = grad_in + taps_f[tap] * dpad[start:start + length]
        wgrad = grad_heads(conv_b, d_recur, head_width)
        rgrad = lax.optimization_barrier(jnp.sum(d_log * (-8.0 * recur_gate), axis=0))
        return (grad_in.astype(jnp.bfloat16), wgrad, rgrad)

    def accumulate(carry, pair):
        grad_in, wgrad, rgrad = one_sequence(pair)
        return ((carry[0] + wgrad, carry[1] + rgrad), grad_in)
    start_carry = (jnp.zeros(weight_a.shape, jnp.float32), jnp.zeros((width,), jnp.float32))
    totals, grad_input = lax.scan(accumulate, start_carry, (branch_in, cotangent))
    return (grad_input, totals[0], totals[1])
```

```python
import jax
import jax.numpy as jnp
from jax import lax
from jax.sharding import PartitionSpec as P

floor_value = 2.5e-07
exact = lax.Precision.HIGHEST


def passed_along(array, axis, by):
    length = lax.axis_size(axis)
    pairs = [(i, i + by) for i in range(length) if 0 <= i + by < length]
    return lax.ppermute(array, axis, pairs)


def mix_heads(values, weights):
    tokens = values.shape[0]
    head_width = weights.shape[0]
    head_count = weights.shape[1] // head_width
    left = values.reshape(tokens, head_count, head_width)
    right = weights.reshape(head_width, head_count, head_width)
    result = jnp.einsum("thk,khj->thj", left, right, preferred_element_type=jnp.float32)
    return result.reshape(tokens, head_count * head_width)


def back_heads(grads, weights):
    tokens = grads.shape[0]
    head_width = weights.shape[0]
    head_count = weights.shape[1] // head_width
    left = grads.reshape(tokens, head_count, head_width)
    right = weights.reshape(head_width, head_count, head_width)
    result = jnp.einsum("thj,khj->thk", left, right, preferred_element_type=jnp.float32)
    return result.reshape(tokens, head_count * head_width)


def grad_heads(values, grads, head_width):
    tokens = values.shape[0]
    head_count = values.shape[1] // head_width
    left = values.reshape(tokens, head_count, head_width)
    right = grads.reshape(tokens, head_count, head_width)
    result = jnp.einsum("thk,thj->khj", left, right, preferred_element_type=jnp.float32)
    return result.reshape(head_width, head_count * head_width)


def compose(own, received):
    return (own[0] * received[0], own[0] * received[1] + own[1])


def block_prefix(forward_item, backward_item, axis):
    span = lax.axis_size(axis)
    ones = jnp.ones_like(forward_item[0])
    zeros = jnp.zeros_like(forward_item[0])
    fwd_incl, fwd_excl = forward_item, (ones, zeros)
    bwd_incl, bwd_excl = backward_item, (ones, zeros)
    shift = 1
    while shift < span:
        got_fwd = passed_along(jnp.stack(fwd_incl), axis, shift)
        got_bwd = passed_along(jnp.stack(bwd_incl), axis, -shift)
        got_fwd = (got_fwd[0], got_fwd[1])
        got_bwd = (got_bwd[0], got_bwd[1])
        fwd_excl = compose(fwd_excl, got_fwd)
        fwd_incl = compose(fwd_incl, got_fwd)
        bwd_excl = compose(bwd_excl, got_bwd)
        bwd_incl = compose(bwd_incl, got_bwd)
        shift *= 2
    return fwd_excl[1], bwd_excl[1]


def on_device(
    branch_in, cotangent, weight_a, weight_x, conv_weight, conv_bias, bias_a, bias_x, rate
):
    inputs = branch_in[0]
    upstream = cotangent[0].astype(jnp.float32)
    length = inputs.shape[0]
    taps = conv_weight.shape[0]
    rows, cols = weight_a.shape
    dp_size = lax.axis_size("dp")
    ctx_size = lax.axis_size("ctx")
    packed = jnp.concatenate(
        [conv_weight, conv_bias[None], bias_a[None], bias_x[None], rate[None]], 0
    )
    param_rows = packed.shape[0]
    both = lax.all_gather(jnp.stack([weight_a, weight_x]), "dp", axis=1, tiled=True)
    head_width = both.shape[1]
    joined = jnp.concatenate([both.reshape(2 * head_width, cols), packed], 0)
    joined = lax.all_gather(joined, "ctx", axis=1, tiled=True)
    full_a = joined[:head_width]
    full_x = joined[head_width : 2 * head_width]
    params = joined[2 * head_width :]
    params = params.astype(jnp.float32)
    taps_f = params[:taps]
    cbias = params[taps]
    abias = params[taps + 1]
    xbias = params[taps + 2]
    rates = params[taps + 3]
    width = params.shape[1]
    tail = passed_along(inputs[length - (taps - 1) :], "ctx", 1)
    padded = jnp.concatenate([tail, inputs], 0).astype(jnp.float32)
    conv = cbias
    for tap in range(taps):
        conv = conv + taps_f[tap] * padded[tap : tap + length]
    conv_b = conv.astype(jnp.bfloat16)
    conv_f = conv_b.astype(jnp.float32)
    recur_gate = jax.nn.sigmoid(mix_heads(conv_b, full_a) + abias)
    input_gate = jax.nn.sigmoid(mix_heads(conv_b, full_x) + xbias)
    log_decay = -8.0 * recur_gate * rates
    decay = jnp.exp(log_decay)
    one_minus = -jnp.expm1(2.0 * log_decay)
    multiplier = jnp.sqrt(jnp.maximum(one_minus, floor_value))
    drive = multiplier * input_gate * conv_f

    row_id = lax.broadcasted_iota(jnp.int32, (length, length), 0)
    col_id = lax.broadcasted_iota(jnp.int32, (length, length), 1)
    lower = (row_id >= col_id).astype(jnp.float32)
    upper = (row_id <= col_id).astype(jnp.float32)
    cum_log = jnp.dot(lower, log_decay, precision=exact)
    grow = jnp.exp(cum_log)
    shrink = jnp.exp(-cum_log)
    local_hidden = grow * jnp.dot(lower, shrink * drive, precision=exact)
    weighted_back = jnp.dot(upper, grow * upstream, precision=exact)
    local_back = shrink * weighted_back
    block_decay = grow[-1]
    state_in, back_in = block_prefix(
        (block_decay, local_hidden[-1]), (block_decay, weighted_back[0]), "ctx"
    )
    hidden = local_hidden + grow * state_in
    previous = jnp.concatenate([state_in[None], hidden[:-1]], 0)
    back = local_back + (block_decay * shrink) * back_in
    slope = jnp.where(one_minus > floor_value, 0.5 / multiplier, 0.0)
    d_mult = back * input_gate * conv_f
    d_log = back * previous * decay - 2.0 * decay * decay * d_mult * slope
    d_recur = (d_log * (-8.0 * rates) * recur_gate * (1.0 - recur_gate)).astype(jnp.bfloat16)
    d_input = (back * multiplier * conv_f * input_gate * (1.0 - input_gate)).astype(jnp.bfloat16)
    d_conv = (
        back * multiplier * input_gate + back_heads(d_recur, full_a) + back_heads(d_input, full_x)
    )
    following = passed_along(d_conv[: taps - 1], "ctx", -1)
    dpad = jnp.concatenate([d_conv, following], 0)
    grad_in = jnp.zeros((length, width), jnp.float32)
    for tap in range(taps):
        start = taps - 1 - tap
        grad_in = grad_in + taps_f[tap] * dpad[start : start + length]
    local_wgrad = grad_heads(conv_b, d_recur, head_width)
    row_part = lax.psum_scatter(local_wgrad, "dp", scatter_dimension=0, tiled=True)
    wgrad = lax.psum_scatter(row_part, "ctx", scatter_dimension=1, tiled=True)
    rgrad = lax.psum(jnp.sum(d_log * (-8.0 * recur_gate), axis=0), ("dp", "ctx"))
    return (grad_in.astype(jnp.bfloat16)[None], wgrad, rgrad)


def solution(mesh):
    placed = (
        P("dp", "ctx", None),
        P("dp", "ctx", None),
        P("dp", "ctx"),
        P("dp", "ctx"),
        P(None, "ctx"),
        P("ctx"),
        P("ctx"),
        P("ctx"),
        P("ctx"),
    )
    return jax.shard_map(
        on_device,
        mesh=mesh,
        in_specs=placed,
        out_specs=(P("dp", "ctx", None), P("dp", "ctx"), P()),
        check_vma=False,
    )
```

```python
import jax
import jax.numpy as jnp
from jax import lax
from jax.sharding import PartitionSpec as P

floor_value = 2.5e-07
exact = lax.Precision.HIGHEST


def passed_along(array, axis, by):
    length = lax.axis_size(axis)
    pairs = [(i, i + by) for i in range(length) if 0 <= i + by < length]
    return lax.ppermute(array, axis, pairs)


def mix_heads(values, weights):
    tokens = values.shape[0]
    head_width = weights.shape[0]
    head_count = weights.shape[1] // head_width
    left = values.reshape(tokens, head_count, head_width)
    right = weights.reshape(head_width, head_count, head_width)
    result = jnp.einsum("thk,khj->thj", left, right, preferred_element_type=jnp.float32)
    return result.reshape(tokens, head_count * head_width)


def back_heads(grads, weights):
    tokens = grads.shape[0]
    head_width = weights.shape[0]
    head_count = weights.shape[1] // head_width
    left = grads.reshape(tokens, head_count, head_width)
    right = weights.reshape(head_width, head_count, head_width)
    result = jnp.einsum("thj,khj->thk", left, right, preferred_element_type=jnp.float32)
    return result.reshape(tokens, head_count * head_width)


def grad_heads(values, grads, head_width):
    tokens = values.shape[0]
    head_count = values.shape[1] // head_width
    left = values.reshape(tokens, head_count, head_width)
    right = grads.reshape(tokens, head_count, head_width)
    result = jnp.einsum("thk,thj->khj", left, right, preferred_element_type=jnp.float32)
    return result.reshape(head_width, head_count * head_width)


def compose(own, received):
    return (own[0] * received[0], own[0] * received[1] + own[1])


def block_prefix(forward_item, backward_item, axis):
    span = lax.axis_size(axis)
    ones = jnp.ones_like(forward_item[0])
    zeros = jnp.zeros_like(forward_item[0])
    fwd_incl, fwd_excl = forward_item, (ones, zeros)
    bwd_incl, bwd_excl = backward_item, (ones, zeros)
    shift = 1
    while shift < span:
        got_fwd = passed_along(jnp.stack(fwd_incl), axis, shift)
        got_bwd = passed_along(jnp.stack(bwd_incl), axis, -shift)
        got_fwd = (got_fwd[0], got_fwd[1])
        got_bwd = (got_bwd[0], got_bwd[1])
        fwd_excl = compose(fwd_excl, got_fwd)
        fwd_incl = compose(fwd_incl, got_fwd)
        bwd_excl = compose(bwd_excl, got_bwd)
        bwd_incl = compose(bwd_incl, got_bwd)
        shift *= 2
    return fwd_excl[1], bwd_excl[1]


def summed_apart(parts, shared, axis):
    count, size = parts.shape
    stacked = jnp.concatenate(
        [parts, jnp.broadcast_to(shared[None], (count, shared.shape[0]))], 1
    )
    sublanes = 8
    total = stacked.shape[1]
    tile = sublanes * 256
    padded = -(-total // tile) * tile
    stacked = jnp.pad(stacked, ((0, 0), (0, padded - total)))
    stacked = stacked.reshape(count * sublanes, padded // sublanes)
    mine = lax.psum_scatter(stacked, axis, scatter_dimension=0, tiled=True).reshape(-1)
    return mine[:size], mine[size:total]


def on_device(
    branch_in, cotangent, weight_a, weight_x, conv_weight, conv_bias, bias_a, bias_x, rate
):
    inputs = branch_in[0]
    upstream = cotangent[0].astype(jnp.float32)
    length = inputs.shape[0]
    taps = conv_weight.shape[0]
    rows, cols = weight_a.shape
    dp_size = lax.axis_size("dp")
    ctx_size = lax.axis_size("ctx")
    packed = jnp.concatenate(
        [conv_weight, conv_bias[None], bias_a[None], bias_x[None], rate[None]], 0
    )
    both = lax.all_gather(jnp.concatenate([weight_a, weight_x], 0), "dp", axis=0, tiled=True)
    both = both.reshape(dp_size, 2, rows, cols).transpose(1, 0, 2, 3)
    head_width = dp_size * rows
    joined = jnp.concatenate([both.reshape(2 * head_width, cols), packed], 0)
    joined = lax.all_gather(joined, "ctx", axis=0, tiled=True)
    joined = joined.reshape(ctx_size, -1, cols).transpose(1, 0, 2).reshape(-1, ctx_size * cols)
    full_a = joined[:head_width]
    full_x = joined[head_width : 2 * head_width]
    params = joined[2 * head_width :]
    params = params.astype(jnp.float32)
    taps_f = params[:taps]
    cbias = params[taps]
    abias = params[taps + 1]
    xbias = params[taps + 2]
    rates = params[taps + 3]
    width = params.shape[1]
    tail = passed_along(inputs[length - (taps - 1) :], "ctx", 1)
    padded = jnp.concatenate([tail, inputs], 0).astype(jnp.float32)
    conv = cbias
    for tap in range(taps):
        conv = conv + taps_f[tap] * padded[tap : tap + length]
    conv_b = conv.astype(jnp.bfloat16)
    conv_f = conv_b.astype(jnp.float32)
    recur_gate = jax.nn.sigmoid(mix_heads(conv_b, full_a) + abias)
    input_gate = jax.nn.sigmoid(mix_heads(conv_b, full_x) + xbias)
    log_decay = -8.0 * recur_gate * rates
    decay = jnp.exp(log_decay)
    one_minus = -jnp.expm1(2.0 * log_decay)
    multiplier = jnp.sqrt(jnp.maximum(one_minus, floor_value))
    drive = multiplier * input_gate * conv_f

    row_id = lax.broadcasted_iota(jnp.int32, (length, length), 0)
    col_id = lax.broadcasted_iota(jnp.int32, (length, length), 1)
    lower = (row_id >= col_id).astype(jnp.float32)
    upper = (row_id <= col_id).astype(jnp.float32)
    cum_log = jnp.dot(lower, log_decay, precision=exact)
    grow = jnp.exp(cum_log)
    shrink = jnp.exp(-cum_log)
    local_hidden = grow * jnp.dot(lower, shrink * drive, precision=exact)
    weighted_back = jnp.dot(upper, grow * upstream, precision=exact)
    local_back = shrink * weighted_back
    block_decay = grow[-1]
    state_in, back_in = block_prefix(
        (block_decay, local_hidden[-1]), (block_decay, weighted_back[0]), "ctx"
    )
    hidden = local_hidden + grow * state_in
    previous = jnp.concatenate([state_in[None], hidden[:-1]], 0)
    back = local_back + (block_decay * shrink) * back_in
    slope = jnp.where(one_minus > floor_value, 0.5 / multiplier, 0.0)
    d_mult = back * input_gate * conv_f
    d_log = back * previous * decay - 2.0 * decay * decay * d_mult * slope
    d_recur = (d_log * (-8.0 * rates) * recur_gate * (1.0 - recur_gate)).astype(jnp.bfloat16)
    d_input = (back * multiplier * conv_f * input_gate * (1.0 - input_gate)).astype(jnp.bfloat16)
    d_conv = (
        back * multiplier * input_gate + back_heads(d_recur, full_a) + back_heads(d_input, full_x)
    )
    following = passed_along(d_conv[: taps - 1], "ctx", -1)
    dpad = jnp.concatenate([d_conv, following], 0)
    grad_in = jnp.zeros((length, width), jnp.float32)
    for tap in range(taps):
        start = taps - 1 - tap
        grad_in = grad_in + taps_f[tap] * dpad[start : start + length]
    local_wgrad = grad_heads(conv_b, d_recur, head_width)
    local_rgrad = jnp.sum(d_log * (-8.0 * recur_gate), axis=0)
    by_channel = local_wgrad.reshape(head_width, ctx_size, cols).transpose(1, 0, 2)
    channel_sum, rgrad = summed_apart(by_channel.reshape(ctx_size, -1), local_rgrad, "ctx")
    by_row = channel_sum.reshape(dp_size, rows * cols)
    row_sum, rgrad = summed_apart(by_row, rgrad, "dp")
    wgrad = row_sum.reshape(rows, cols)
    return (grad_in.astype(jnp.bfloat16)[None], wgrad, rgrad)


def solution(mesh):
    placed = (
        P("dp", "ctx", None),
        P("dp", "ctx", None),
        P("dp", "ctx"),
        P("dp", "ctx"),
        P(None, "ctx"),
        P("ctx"),
        P("ctx"),
        P("ctx"),
        P("ctx"),
    )
    return jax.shard_map(
        on_device,
        mesh=mesh,
        in_specs=placed,
        out_specs=(P("dp", "ctx", None), P("dp", "ctx"), P()),
        check_vma=False,
    )
```

```python
import jax
import jax.numpy as jnp
from jax import lax
from jax.sharding import PartitionSpec as P

floor_value = 2.5e-07
exact = lax.Precision.HIGHEST


def passed_along(array, axis, by):
    length = lax.axis_size(axis)
    pairs = [(i, i + by) for i in range(length) if 0 <= i + by < length]
    return lax.ppermute(array, axis, pairs)


def mix_heads(values, weights):
    tokens = values.shape[0]
    head_width = weights.shape[0]
    head_count = weights.shape[1] // head_width
    left = values.reshape(tokens, head_count, head_width)
    right = weights.reshape(head_width, head_count, head_width)
    result = jnp.einsum("thk,khj->thj", left, right, preferred_element_type=jnp.float32)
    return result.reshape(tokens, head_count * head_width)


def back_heads(grads, weights):
    tokens = grads.shape[0]
    head_width = weights.shape[0]
    head_count = weights.shape[1] // head_width
    left = grads.reshape(tokens, head_count, head_width)
    right = weights.reshape(head_width, head_count, head_width)
    result = jnp.einsum("thj,khj->thk", left, right, preferred_element_type=jnp.float32)
    return result.reshape(tokens, head_count * head_width)


def grad_heads(values, grads, head_width):
    tokens = values.shape[0]
    head_count = values.shape[1] // head_width
    left = values.reshape(tokens, head_count, head_width)
    right = grads.reshape(tokens, head_count, head_width)
    result = jnp.einsum("thk,thj->khj", left, right, preferred_element_type=jnp.float32)
    return result.reshape(head_width, head_count * head_width)


def compose(own, received):
    return (own[0] * received[0], own[0] * received[1] + own[1])


def block_prefix(forward_item, backward_item, axis):
    span = lax.axis_size(axis)
    ones = jnp.ones_like(forward_item[0])
    zeros = jnp.zeros_like(forward_item[0])
    fwd_incl, fwd_excl = forward_item, (ones, zeros)
    bwd_incl, bwd_excl = backward_item, (ones, zeros)
    shift = 1
    while shift < span:
        got_fwd = passed_along(jnp.stack(fwd_incl), axis, shift)
        got_bwd = passed_along(jnp.stack(bwd_incl), axis, -shift)
        got_fwd = (got_fwd[0], got_fwd[1])
        got_bwd = (got_bwd[0], got_bwd[1])
        fwd_excl = compose(fwd_excl, got_fwd)
        fwd_incl = compose(fwd_incl, got_fwd)
        bwd_excl = compose(bwd_excl, got_bwd)
        bwd_incl = compose(bwd_incl, got_bwd)
        shift *= 2
    return fwd_excl[1], bwd_excl[1]


def exchanged(array, axis, stride):
    length = lax.axis_size(axis)
    return lax.ppermute(array, axis, [(i, i ^ stride) for i in range(length)])


def gathered_by_doubling(piece, axis):
    length = lax.axis_size(axis)
    me = lax.axis_index(axis)
    held = piece[None]
    stride = 1
    while stride < length:
        got = exchanged(held, axis, stride)
        upper = (me // stride) % 2 == 1
        low = jnp.where(upper, got, held)
        high = jnp.where(upper, held, got)
        held = jnp.concatenate([low, high], 0)
        stride *= 2
    return held


def summed_by_halving(blocks, axis):
    length = lax.axis_size(axis)
    me = lax.axis_index(axis)
    held = blocks
    stride = length // 2
    while stride >= 1:
        halves = held.reshape((2, held.shape[0] // 2) + held.shape[1:])
        upper = ((me // stride) % 2).astype(jnp.int32)
        keep = lax.dynamic_index_in_dim(halves, upper, 0, keepdims=False)
        give = lax.dynamic_index_in_dim(halves, 1 - upper, 0, keepdims=False)
        held = keep + exchanged(give, axis, stride)
        stride //= 2
    return held[0]


def summed_apart(parts, shared, axis):
    count, size = parts.shape
    stacked = jnp.concatenate(
        [parts, jnp.broadcast_to(shared[None], (count, shared.shape[0]))], 1
    )
    mine = summed_by_halving(stacked, axis)
    return mine[:size], mine[size:]

def on_device(
    branch_in, cotangent, weight_a, weight_x, conv_weight, conv_bias, bias_a, bias_x, rate
):
    inputs = branch_in[0]
    upstream = cotangent[0].astype(jnp.float32)
    length = inputs.shape[0]
    taps = conv_weight.shape[0]
    rows, cols = weight_a.shape
    dp_size = lax.axis_size("dp")
    ctx_size = lax.axis_size("ctx")
    packed = jnp.concatenate(
        [conv_weight, conv_bias[None], bias_a[None], bias_x[None], rate[None]], 0
    )
    both = lax.all_gather(jnp.concatenate([weight_a, weight_x], 0), "dp", axis=0, tiled=True)
    both = both.reshape(dp_size, 2, rows, cols).transpose(1, 0, 2, 3)
    head_width = dp_size * rows
    joined = jnp.concatenate([both.reshape(2 * head_width, cols), packed], 0)
    joined = gathered_by_doubling(joined, "ctx")
    joined = joined.transpose(1, 0, 2).reshape(-1, ctx_size * cols)
    full_a = joined[:head_width]
    full_x = joined[head_width : 2 * head_width]
    params = joined[2 * head_width :]
    params = params.astype(jnp.float32)
    taps_f = params[:taps]
    cbias = params[taps]
    abias = params[taps + 1]
    xbias = params[taps + 2]
    rates = params[taps + 3]
    width = params.shape[1]
    tail = passed_along(inputs[length - (taps - 1) :], "ctx", 1)
    padded = jnp.concatenate([tail, inputs], 0).astype(jnp.float32)
    conv = cbias
    for tap in range(taps):
        conv = conv + taps_f[tap] * padded[tap : tap + length]
    conv_b = conv.astype(jnp.bfloat16)
    conv_f = conv_b.astype(jnp.float32)
    recur_gate = jax.nn.sigmoid(mix_heads(conv_b, full_a) + abias)
    input_gate = jax.nn.sigmoid(mix_heads(conv_b, full_x) + xbias)
    log_decay = -8.0 * recur_gate * rates
    decay = jnp.exp(log_decay)
    one_minus = -jnp.expm1(2.0 * log_decay)
    multiplier = jnp.sqrt(jnp.maximum(one_minus, floor_value))
    drive = multiplier * input_gate * conv_f

    row_id = lax.broadcasted_iota(jnp.int32, (length, length), 0)
    col_id = lax.broadcasted_iota(jnp.int32, (length, length), 1)
    lower = (row_id >= col_id).astype(jnp.float32)
    upper = (row_id <= col_id).astype(jnp.float32)
    cum_log = jnp.dot(lower, log_decay, precision=exact)
    grow = jnp.exp(cum_log)
    shrink = jnp.exp(-cum_log)
    local_hidden = grow * jnp.dot(lower, shrink * drive, precision=exact)
    weighted_back = jnp.dot(upper, grow * upstream, precision=exact)
    local_back = shrink * weighted_back
    block_decay = grow[-1]
    state_in, back_in = block_prefix(
        (block_decay, local_hidden[-1]), (block_decay, weighted_back[0]), "ctx"
    )
    hidden = local_hidden + grow * state_in
    previous = jnp.concatenate([state_in[None], hidden[:-1]], 0)
    back = local_back + (block_decay * shrink) * back_in
    slope = jnp.where(one_minus > floor_value, 0.5 / multiplier, 0.0)
    d_mult = back * input_gate * conv_f
    d_log = back * previous * decay - 2.0 * decay * decay * d_mult * slope
    d_recur = (d_log * (-8.0 * rates) * recur_gate * (1.0 - recur_gate)).astype(jnp.bfloat16)
    d_input = (back * multiplier * conv_f * input_gate * (1.0 - input_gate)).astype(jnp.bfloat16)
    d_conv = (
        back * multiplier * input_gate + back_heads(d_recur, full_a) + back_heads(d_input, full_x)
    )
    following = passed_along(d_conv[: taps - 1], "ctx", -1)
    dpad = jnp.concatenate([d_conv, following], 0)
    grad_in = jnp.zeros((length, width), jnp.float32)
    for tap in range(taps):
        start = taps - 1 - tap
        grad_in = grad_in + taps_f[tap] * dpad[start : start + length]
    local_wgrad = grad_heads(conv_b, d_recur, head_width)
    local_rgrad = jnp.sum(d_log * (-8.0 * recur_gate), axis=0)
    by_channel = local_wgrad.reshape(head_width, ctx_size, cols).transpose(1, 0, 2)
    channel_sum, rgrad = summed_apart(by_channel.reshape(ctx_size, -1), local_rgrad, "ctx")
    by_row = channel_sum.reshape(dp_size, rows * cols)
    row_sum, rgrad = summed_apart(by_row, rgrad, "dp")
    wgrad = row_sum.reshape(rows, cols)
    return (grad_in.astype(jnp.bfloat16)[None], wgrad, rgrad)


def solution(mesh):
    placed = (
        P("dp", "ctx", None),
        P("dp", "ctx", None),
        P("dp", "ctx"),
        P("dp", "ctx"),
        P(None, "ctx"),
        P("ctx"),
        P("ctx"),
        P("ctx"),
        P("ctx"),
    )
    return jax.shard_map(
        on_device,
        mesh=mesh,
        in_specs=placed,
        out_specs=(P("dp", "ctx", None), P("dp", "ctx"), P()),
        check_vma=False,
    )
```

```python
import jax
import jax.numpy as jnp
from jax import lax
from jax.sharding import PartitionSpec as P

floor_value = 2.5e-07
exact = lax.Precision.HIGHEST


def passed_along(array, axis, by):
    length = lax.axis_size(axis)
    pairs = [(i, i + by) for i in range(length) if 0 <= i + by < length]
    return lax.ppermute(array, axis, pairs)


def mix_heads(values, weights):
    tokens = values.shape[0]
    head_width = weights.shape[0]
    head_count = weights.shape[1] // head_width
    left = values.reshape(tokens, head_count, head_width)
    right = weights.reshape(head_width, head_count, head_width)
    result = jnp.einsum("thk,khj->thj", left, right, preferred_element_type=jnp.float32)
    return result.reshape(tokens, head_count * head_width)


def back_heads(grads, weights):
    tokens = grads.shape[0]
    head_width = weights.shape[0]
    head_count = weights.shape[1] // head_width
    left = grads.reshape(tokens, head_count, head_width)
    right = weights.reshape(head_width, head_count, head_width)
    result = jnp.einsum("thj,khj->thk", left, right, preferred_element_type=jnp.float32)
    return result.reshape(tokens, head_count * head_width)


def grad_heads(values, grads, head_width):
    tokens = values.shape[0]
    head_count = values.shape[1] // head_width
    left = values.reshape(tokens, head_count, head_width)
    right = grads.reshape(tokens, head_count, head_width)
    result = jnp.einsum("thk,thj->khj", left, right, preferred_element_type=jnp.float32)
    return result.reshape(head_width, head_count * head_width)


def compose(own, received):
    return (own[0] * received[0], own[0] * received[1] + own[1])


def block_prefix(forward_item, backward_item, axis):
    span = lax.axis_size(axis)
    ones = jnp.ones_like(forward_item[0])
    zeros = jnp.zeros_like(forward_item[0])
    fwd_incl, fwd_excl = forward_item, (ones, zeros)
    bwd_incl, bwd_excl = backward_item, (ones, zeros)
    shift = 1
    while shift < span:
        got_fwd = passed_along(jnp.stack(fwd_incl), axis, shift)
        got_bwd = passed_along(jnp.stack(bwd_incl), axis, -shift)
        got_fwd = (got_fwd[0], got_fwd[1])
        got_bwd = (got_bwd[0], got_bwd[1])
        fwd_excl = compose(fwd_excl, got_fwd)
        fwd_incl = compose(fwd_incl, got_fwd)
        bwd_excl = compose(bwd_excl, got_bwd)
        bwd_incl = compose(bwd_incl, got_bwd)
        shift *= 2
    return fwd_excl[1], bwd_excl[1]


def low_first(length):
    strides = []
    stride = 1
    while stride < length:
        strides.append(stride)
        stride *= 2
    return strides


def exchanged(array, axis, stride):
    length = lax.axis_size(axis)
    return lax.ppermute(array, axis, [(i, i ^ stride) for i in range(length)])


def gathered_by_doubling(piece, axis, strides):
    length = lax.axis_size(axis)
    me = lax.axis_index(axis)
    held = piece
    for count, stride in enumerate(strides):
        got = exchanged(held, axis, stride)
        upper = (me // stride) % 2 == 1
        low = jnp.where(upper, got, held)
        high = jnp.where(upper, held, got)
        held = jnp.stack([low, high], count)
    rounds = len(strides)
    order = sorted(range(rounds), key=lambda j: -strides[j])
    held = held.transpose(order + list(range(rounds, held.ndim)))
    return held.reshape((length,) + piece.shape)


def summed_by_halving(blocks, axis, strides):
    length = lax.axis_size(axis)
    me = lax.axis_index(axis)
    bits = []
    stride = length // 2
    while stride >= 1:
        bits.append(stride)
        stride //= 2
    held = blocks.reshape((2,) * len(bits) + blocks.shape[1:])
    for stride in strides:
        place = bits.index(stride)
        upper = ((me // stride) % 2).astype(jnp.int32)
        keep = lax.dynamic_index_in_dim(held, upper, place, keepdims=False)
        give = lax.dynamic_index_in_dim(held, 1 - upper, place, keepdims=False)
        held = keep + exchanged(give, axis, stride)
        bits.remove(stride)
    return held

def summed_apart(parts, shared, axis, strides):
    count, size = parts.shape
    stacked = jnp.concatenate(
        [parts, jnp.broadcast_to(shared[None], (count, shared.shape[0]))], 1
    )
    mine = summed_by_halving(stacked, axis, strides)
    return mine[:size], mine[size:]

def on_device(
    branch_in, cotangent, weight_a, weight_x, conv_weight, conv_bias, bias_a, bias_x, rate
):
    inputs = branch_in[0]
    upstream = cotangent[0].astype(jnp.float32)
    length = inputs.shape[0]
    taps = conv_weight.shape[0]
    rows, cols = weight_a.shape
    dp_size = lax.axis_size("dp")
    ctx_size = lax.axis_size("ctx")
    packed = jnp.concatenate(
        [conv_weight, conv_bias[None], bias_a[None], bias_x[None], rate[None]], 0
    )
    width = ctx_size * cols
    joined = jnp.concatenate([weight_a, weight_x, packed], 0)
    by_ctx = gathered_by_doubling(joined, "ctx", low_first(ctx_size))
    by_ctx = by_ctx.transpose(1, 0, 2).reshape(joined.shape[0], width)
    params = by_ctx[2 * rows :]
    by_dp = gathered_by_doubling(by_ctx[: 2 * rows], "dp", low_first(dp_size)[::-1])
    full_a = by_dp[:, :rows].reshape(dp_size * rows, width)
    full_x = by_dp[:, rows:].reshape(dp_size * rows, width)
    head_width = dp_size * rows
    params = params.astype(jnp.float32)
    taps_f = params[:taps]
    cbias = params[taps]
    abias = params[taps + 1]
    xbias = params[taps + 2]
    rates = params[taps + 3]
    tail = passed_along(inputs[length - (taps - 1) :], "ctx", 1)
    padded = jnp.concatenate([tail, inputs], 0).astype(jnp.float32)
    conv = cbias
    for tap in range(taps):
        conv = conv + taps_f[tap] * padded[tap : tap + length]
    conv_b = conv.astype(jnp.bfloat16)
    conv_f = conv_b.astype(jnp.float32)
    recur_gate = jax.nn.sigmoid(mix_heads(conv_b, full_a) + abias)
    input_gate = jax.nn.sigmoid(mix_heads(conv_b, full_x) + xbias)
    log_decay = -8.0 * recur_gate * rates
    decay = jnp.exp(log_decay)
    one_minus = -jnp.expm1(2.0 * log_decay)
    multiplier = jnp.sqrt(jnp.maximum(one_minus, floor_value))
    drive = multiplier * input_gate * conv_f

    row_id = lax.broadcasted_iota(jnp.int32, (length, length), 0)
    col_id = lax.broadcasted_iota(jnp.int32, (length, length), 1)
    lower = (row_id >= col_id).astype(jnp.float32)
    upper = (row_id <= col_id).astype(jnp.float32)
    cum_log = jnp.dot(lower, log_decay, precision=exact)
    grow = jnp.exp(cum_log)
    shrink = jnp.exp(-cum_log)
    local_hidden = grow * jnp.dot(lower, shrink * drive, precision=exact)
    weighted_back = jnp.dot(upper, grow * upstream, precision=exact)
    local_back = shrink * weighted_back
    block_decay = grow[-1]
    state_in, back_in = block_prefix(
        (block_decay, local_hidden[-1]), (block_decay, weighted_back[0]), "ctx"
    )
    hidden = local_hidden + grow * state_in
    previous = jnp.concatenate([state_in[None], hidden[:-1]], 0)
    back = local_back + (block_decay * shrink) * back_in
    slope = jnp.where(one_minus > floor_value, 0.5 / multiplier, 0.0)
    d_mult = back * input_gate * conv_f
    d_log = back * previous * decay - 2.0 * decay * decay * d_mult * slope
    d_recur = (d_log * (-8.0 * rates) * recur_gate * (1.0 - recur_gate)).astype(jnp.bfloat16)
    d_input = (back * multiplier * conv_f * input_gate * (1.0 - input_gate)).astype(jnp.bfloat16)
    d_conv = (
        back * multiplier * input_gate + back_heads(d_recur, full_a) + back_heads(d_input, full_x)
    )
    following = passed_along(d_conv[: taps - 1], "ctx", -1)
    dpad = jnp.concatenate([d_conv, following], 0)
    grad_in = jnp.zeros((length, width), jnp.float32)
    for tap in range(taps):
        start = taps - 1 - tap
        grad_in = grad_in + taps_f[tap] * dpad[start : start + length]
    local_wgrad = grad_heads(conv_b, d_recur, head_width)
    local_rgrad = jnp.sum(d_log * (-8.0 * recur_gate), axis=0)
    by_row = local_wgrad.reshape(dp_size, rows * width)
    row_sum, rgrad = summed_apart(by_row, local_rgrad, "dp", low_first(dp_size))
    by_channel = row_sum.reshape(rows, ctx_size, cols).transpose(1, 0, 2)
    channel_sum, rgrad = summed_apart(
        by_channel.reshape(ctx_size, rows * cols), rgrad, "ctx", low_first(ctx_size)
    )
    wgrad = channel_sum.reshape(rows, cols)
    return (grad_in.astype(jnp.bfloat16)[None], wgrad, rgrad)


def solution(mesh):
    placed = (
        P("dp", "ctx", None),
        P("dp", "ctx", None),
        P("dp", "ctx"),
        P("dp", "ctx"),
        P(None, "ctx"),
        P("ctx"),
        P("ctx"),
        P("ctx"),
        P("ctx"),
    )
    return jax.shard_map(
        on_device,
        mesh=mesh,
        in_specs=placed,
        out_specs=(P("dp", "ctx", None), P("dp", "ctx"), P()),
        check_vma=False,
    )
```

```python
import jax
import jax.numpy as jnp
from jax import lax
from jax.sharding import PartitionSpec as P

floor_value = 2.5e-07
exact = lax.Precision.HIGHEST


def passed_along(array, axis, by):
    length = lax.axis_size(axis)
    pairs = [(i, i + by) for i in range(length) if 0 <= i + by < length]
    return lax.ppermute(array, axis, pairs)


def mix_heads(values, weights):
    tokens = values.shape[0]
    head_width = weights.shape[0]
    head_count = weights.shape[1] // head_width
    left = values.reshape(tokens, head_count, head_width)
    right = weights.reshape(head_width, head_count, head_width)
    result = jnp.einsum("thk,khj->thj", left, right, preferred_element_type=jnp.float32)
    return result.reshape(tokens, head_count * head_width)


def back_heads(grads, weights):
    tokens = grads.shape[0]
    head_width = weights.shape[0]
    head_count = weights.shape[1] // head_width
    left = grads.reshape(tokens, head_count, head_width)
    right = weights.reshape(head_width, head_count, head_width)
    result = jnp.einsum("thj,khj->thk", left, right, preferred_element_type=jnp.float32)
    return result.reshape(tokens, head_count * head_width)


def grad_heads(values, grads, head_width):
    tokens = values.shape[0]
    head_count = values.shape[1] // head_width
    left = values.reshape(tokens, head_count, head_width)
    right = grads.reshape(tokens, head_count, head_width)
    result = jnp.einsum("thk,thj->khj", left, right, preferred_element_type=jnp.float32)
    return result.reshape(head_width, head_count * head_width)


def compose(own, received):
    return (own[0] * received[0], own[0] * received[1] + own[1])


def block_prefix(forward_item, backward_item, axis):
    span = lax.axis_size(axis)
    ones = jnp.ones_like(forward_item[0])
    zeros = jnp.zeros_like(forward_item[0])
    fwd_incl, fwd_excl = forward_item, (ones, zeros)
    bwd_incl, bwd_excl = backward_item, (ones, zeros)
    reach = 1
    while reach < span:
        shifts = [j * reach for j in (1, 2, 3) if j * reach < span]
        fwd_got = [passed_along(jnp.stack(fwd_incl), axis, s) for s in shifts]
        bwd_got = [passed_along(jnp.stack(bwd_incl), axis, -s) for s in shifts]
        fwd_span = (fwd_got[-1][0], fwd_got[-1][1])
        bwd_span = (bwd_got[-1][0], bwd_got[-1][1])
        for got in fwd_got[-2::-1]:
            fwd_span = compose((got[0], got[1]), fwd_span)
        for got in bwd_got[-2::-1]:
            bwd_span = compose((got[0], got[1]), bwd_span)
        fwd_excl = compose(fwd_excl, fwd_span)
        fwd_incl = compose(fwd_incl, fwd_span)
        bwd_excl = compose(bwd_excl, bwd_span)
        bwd_incl = compose(bwd_incl, bwd_span)
        reach *= 4
    return fwd_excl[1], bwd_excl[1]

def digit_steps(length):
    bits = []
    stride = 1
    while stride < length:
        bits.append(stride)
        stride *= 2
    return [bits[i : i + 2] for i in range(0, len(bits), 2)]


def exchanged(array, axis, mask):
    length = lax.axis_size(axis)
    return lax.ppermute(array, axis, [(i, i ^ mask) for i in range(length)])


def patterns(step):
    masks = [0]
    for stride in step:
        masks = masks + [m + stride for m in masks]
    return masks


def digit_of(me, step):
    value = jnp.int32(0)
    for place, stride in enumerate(step):
        value = value + ((me // stride) % 2) * (2**place)
    return value


def mask_of(pattern_index, step):
    mask = 0
    for place, stride in enumerate(step):
        if (pattern_index >> place) & 1:
            mask += stride
    return mask


def gathered_by_doubling(piece, axis, steps):
    length = lax.axis_size(axis)
    me = lax.axis_index(axis)
    held = piece
    done = 0
    order = []
    for step in steps:
        size = 2 ** len(step)
        mine = digit_of(me, step)
        sources = [held] + [exchanged(held, axis, mask_of(p, step)) for p in range(1, size)]
        pool = jnp.stack(sources, 0)
        slots = [
            lax.dynamic_index_in_dim(pool, jnp.bitwise_xor(mine, v), 0, keepdims=False)
            for v in range(size)
        ]
        held = jnp.stack(slots, done)
        held = held.reshape(held.shape[:done] + (2,) * len(step) + held.shape[done + 1 :])
        order = order + step[::-1]
        done += len(step)
    rank = sorted(range(done), key=lambda j: -order[j])
    held = held.transpose(rank + list(range(done, held.ndim)))
    return held.reshape((length,) + piece.shape)


def summed_by_halving(blocks, axis, steps):
    length = lax.axis_size(axis)
    me = lax.axis_index(axis)
    bits = []
    stride = length // 2
    while stride >= 1:
        bits.append(stride)
        stride //= 2
    held = blocks
    for step in steps:
        size = 2 ** len(step)
        mine = digit_of(me, step)
        rest = [b for b in bits if b not in step]
        front = held.reshape((2,) * len(bits) + blocks.shape[1:]) if bits else held
        lead = [bits.index(b) for b in step[::-1]] + [bits.index(b) for b in rest]
        front = front.transpose(lead + list(range(len(bits), front.ndim)))
        front = front.reshape((size,) + (2 ** len(rest),) + blocks.shape[1:])
        total = lax.dynamic_index_in_dim(front, mine, 0, keepdims=False)
        for p in range(1, size):
            give = lax.dynamic_index_in_dim(front, jnp.bitwise_xor(mine, p), 0, keepdims=False)
            total = total + exchanged(give, axis, mask_of(p, step))
        held = total
        bits = rest
    return held[0]

def summed_apart(parts, shared, axis, strides):
    count, size = parts.shape
    stacked = jnp.concatenate(
        [parts, jnp.broadcast_to(shared[None], (count, shared.shape[0]))], 1
    )
    mine = summed_by_halving(stacked, axis, strides)
    return mine[:size], mine[size:]

def on_device(
    branch_in, cotangent, weight_a, weight_x, conv_weight, conv_bias, bias_a, bias_x, rate
):
    inputs = branch_in[0]
    upstream = cotangent[0].astype(jnp.float32)
    length = inputs.shape[0]
    taps = conv_weight.shape[0]
    rows, cols = weight_a.shape
    dp_size = lax.axis_size("dp")
    ctx_size = lax.axis_size("ctx")
    packed = jnp.concatenate(
        [conv_weight, conv_bias[None], bias_a[None], bias_x[None], rate[None]], 0
    )
    width = ctx_size * cols
    joined = jnp.concatenate([weight_a, weight_x, packed], 0)
    by_ctx = gathered_by_doubling(joined, "ctx", digit_steps(ctx_size))
    by_ctx = by_ctx.transpose(1, 0, 2).reshape(joined.shape[0], width)
    params = by_ctx[2 * rows :]
    by_dp = gathered_by_doubling(by_ctx[: 2 * rows], "dp", digit_steps(dp_size)[::-1])
    full_a = by_dp[:, :rows].reshape(dp_size * rows, width)
    full_x = by_dp[:, rows:].reshape(dp_size * rows, width)
    head_width = dp_size * rows
    params = params.astype(jnp.float32)
    taps_f = params[:taps]
    cbias = params[taps]
    abias = params[taps + 1]
    xbias = params[taps + 2]
    rates = params[taps + 3]
    tail = passed_along(inputs[length - (taps - 1) :], "ctx", 1)
    padded = jnp.concatenate([tail, inputs], 0).astype(jnp.float32)
    conv = cbias
    for tap in range(taps):
        conv = conv + taps_f[tap] * padded[tap : tap + length]
    conv_b = conv.astype(jnp.bfloat16)
    conv_f = conv_b.astype(jnp.float32)
    recur_gate = jax.nn.sigmoid(mix_heads(conv_b, full_a) + abias)
    input_gate = jax.nn.sigmoid(mix_heads(conv_b, full_x) + xbias)
    log_decay = -8.0 * recur_gate * rates
    decay = jnp.exp(log_decay)
    one_minus = -jnp.expm1(2.0 * log_decay)
    multiplier = jnp.sqrt(jnp.maximum(one_minus, floor_value))
    drive = multiplier * input_gate * conv_f

    row_id = lax.broadcasted_iota(jnp.int32, (length, length), 0)
    col_id = lax.broadcasted_iota(jnp.int32, (length, length), 1)
    lower = (row_id >= col_id).astype(jnp.float32)
    upper = (row_id <= col_id).astype(jnp.float32)
    cum_log = jnp.dot(lower, log_decay, precision=exact)
    grow = jnp.exp(cum_log)
    shrink = jnp.exp(-cum_log)
    local_hidden = grow * jnp.dot(lower, shrink * drive, precision=exact)
    weighted_back = jnp.dot(upper, grow * upstream, precision=exact)
    local_back = shrink * weighted_back
    block_decay = grow[-1]
    state_in, back_in = block_prefix(
        (block_decay, local_hidden[-1]), (block_decay, weighted_back[0]), "ctx"
    )
    hidden = local_hidden + grow * state_in
    previous = jnp.concatenate([state_in[None], hidden[:-1]], 0)
    back = local_back + (block_decay * shrink) * back_in
    slope = jnp.where(one_minus > floor_value, 0.5 / multiplier, 0.0)
    d_mult = back * input_gate * conv_f
    d_log = back * previous * decay - 2.0 * decay * decay * d_mult * slope
    d_recur = (d_log * (-8.0 * rates) * recur_gate * (1.0 - recur_gate)).astype(jnp.bfloat16)
    d_input = (back * multiplier * conv_f * input_gate * (1.0 - input_gate)).astype(jnp.bfloat16)
    d_conv = (
        back * multiplier * input_gate + back_heads(d_recur, full_a) + back_heads(d_input, full_x)
    )
    following = passed_along(d_conv[: taps - 1], "ctx", -1)
    dpad = jnp.concatenate([d_conv, following], 0)
    grad_in = jnp.zeros((length, width), jnp.float32)
    for tap in range(taps):
        start = taps - 1 - tap
        grad_in = grad_in + taps_f[tap] * dpad[start : start + length]
    local_wgrad = grad_heads(conv_b, d_recur, head_width)
    local_rgrad = jnp.sum(d_log * (-8.0 * recur_gate), axis=0)
    by_row = local_wgrad.reshape(dp_size, rows * width)
    row_sum, rgrad = summed_apart(by_row, local_rgrad, "dp", digit_steps(dp_size))
    by_channel = row_sum.reshape(rows, ctx_size, cols).transpose(1, 0, 2)
    channel_sum, rgrad = summed_apart(
        by_channel.reshape(ctx_size, rows * cols), rgrad, "ctx", digit_steps(ctx_size)
    )
    wgrad = channel_sum.reshape(rows, cols)
    return (grad_in.astype(jnp.bfloat16)[None], wgrad, rgrad)


def solution(mesh):
    placed = (
        P("dp", "ctx", None),
        P("dp", "ctx", None),
        P("dp", "ctx"),
        P("dp", "ctx"),
        P(None, "ctx"),
        P("ctx"),
        P("ctx"),
        P("ctx"),
        P("ctx"),
    )
    return jax.shard_map(
        on_device,
        mesh=mesh,
        in_specs=placed,
        out_specs=(P("dp", "ctx", None), P("dp", "ctx"), P()),
        check_vma=False,
    )
```

```python
import jax
import jax.numpy as jnp
from jax import lax
from jax.sharding import PartitionSpec as P

floor_value = 2.5e-07
exact = lax.Precision.HIGHEST


def passed_along(array, axis, by):
    length = lax.axis_size(axis)
    pairs = [(i, i + by) for i in range(length) if 0 <= i + by < length]
    return lax.ppermute(array, axis, pairs)


def mix_heads(values, weights):
    tokens = values.shape[0]
    head_width = weights.shape[0]
    head_count = weights.shape[1] // head_width
    left = values.reshape(tokens, head_count, head_width)
    right = weights.reshape(head_width, head_count, head_width)
    result = jnp.einsum("thk,khj->thj", left, right, preferred_element_type=jnp.float32)
    return result.reshape(tokens, head_count * head_width)


def back_heads(grads, weights):
    tokens = grads.shape[0]
    head_width = weights.shape[0]
    head_count = weights.shape[1] // head_width
    left = grads.reshape(tokens, head_count, head_width)
    right = weights.reshape(head_width, head_count, head_width)
    result = jnp.einsum("thj,khj->thk", left, right, preferred_element_type=jnp.float32)
    return result.reshape(tokens, head_count * head_width)


def grad_heads(values, grads, head_width):
    tokens = values.shape[0]
    head_count = values.shape[1] // head_width
    left = values.reshape(tokens, head_count, head_width)
    right = grads.reshape(tokens, head_count, head_width)
    result = jnp.einsum("thk,thj->khj", left, right, preferred_element_type=jnp.float32)
    return result.reshape(head_width, head_count * head_width)


def compose(own, received):
    return (own[0] * received[0], own[0] * received[1] + own[1])


def block_prefix(decay_all, forward_all, backward_all, axis):
    span = lax.axis_size(axis)
    me = lax.axis_index(axis)
    ones = jnp.ones_like(decay_all)
    zeros = jnp.zeros_like(decay_all)
    group = (decay_all, forward_all, backward_all)
    before = (ones, zeros)
    after = (ones, zeros)
    stride = 1
    while stride < span:
        got = exchanged(jnp.stack(group), axis, stride)
        other = (got[0], got[1], got[2])
        right_half = (me // stride) % 2 == 1
        mixed_before = compose(before, (other[0], other[1]))
        mixed_after = compose(after, (other[0], other[2]))
        before = tuple(jnp.where(right_half, n, o) for n, o in zip(mixed_before, before))
        after = tuple(jnp.where(right_half, o, n) for n, o in zip(mixed_after, after))
        forward_total = jnp.where(
            right_half, group[0] * other[1] + group[1], other[0] * group[1] + other[1]
        )
        backward_total = jnp.where(
            right_half, other[0] * group[2] + other[2], group[0] * other[2] + group[2]
        )
        group = (group[0] * other[0], forward_total, backward_total)
        stride *= 2
    return before[1], after[1]

def bit_steps(length):
    return [[stride] for step in digit_steps(length) for stride in step]


def digit_steps(length):
    bits = []
    stride = 1
    while stride < length:
        bits.append(stride)
        stride *= 2
    return [bits[i : i + 2] for i in range(0, len(bits), 2)]


def exchanged(array, axis, mask):
    length = lax.axis_size(axis)
    return lax.ppermute(array, axis, [(i, i ^ mask) for i in range(length)])


def patterns(step):
    masks = [0]
    for stride in step:
        masks = masks + [m + stride for m in masks]
    return masks


def digit_of(me, step):
    value = jnp.int32(0)
    for place, stride in enumerate(step):
        value = value + ((me // stride) % 2) * (2**place)
    return value


def mask_of(pattern_index, step):
    mask = 0
    for place, stride in enumerate(step):
        if (pattern_index >> place) & 1:
            mask += stride
    return mask


def gathered_by_doubling(piece, axis, steps):
    length = lax.axis_size(axis)
    me = lax.axis_index(axis)
    held = piece
    done = 0
    order = []
    for step in steps:
        size = 2 ** len(step)
        mine = digit_of(me, step)
        sources = [held] + [exchanged(held, axis, mask_of(p, step)) for p in range(1, size)]
        pool = jnp.stack(sources, 0)
        slots = [
            lax.dynamic_index_in_dim(pool, jnp.bitwise_xor(mine, v), 0, keepdims=False)
            for v in range(size)
        ]
        held = jnp.stack(slots, done)
        held = held.reshape(held.shape[:done] + (2,) * len(step) + held.shape[done + 1 :])
        order = order + step[::-1]
        done += len(step)
    rank = sorted(range(done), key=lambda j: -order[j])
    held = held.transpose(rank + list(range(done, held.ndim)))
    return held.reshape((length,) + piece.shape)


def summed_by_halving(blocks, axis, steps):
    length = lax.axis_size(axis)
    me = lax.axis_index(axis)
    bits = []
    stride = length // 2
    while stride >= 1:
        bits.append(stride)
        stride //= 2
    held = blocks
    for step in steps:
        size = 2 ** len(step)
        mine = digit_of(me, step)
        rest = [b for b in bits if b not in step]
        front = held.reshape((2,) * len(bits) + blocks.shape[1:]) if bits else held
        lead = [bits.index(b) for b in step[::-1]] + [bits.index(b) for b in rest]
        front = front.transpose(lead + list(range(len(bits), front.ndim)))
        front = front.reshape((size,) + (2 ** len(rest),) + blocks.shape[1:])
        total = lax.dynamic_index_in_dim(front, mine, 0, keepdims=False)
        for p in range(1, size):
            give = lax.dynamic_index_in_dim(front, jnp.bitwise_xor(mine, p), 0, keepdims=False)
            total = total + exchanged(give, axis, mask_of(p, step))
        held = total
        bits = rest
    return held[0]

def summed_apart(parts, shared, axis, strides):
    count, size = parts.shape
    stacked = jnp.concatenate(
        [parts, jnp.broadcast_to(shared[None], (count, shared.shape[0]))], 1
    )
    mine = summed_by_halving(stacked, axis, strides)
    return mine[:size], mine[size:]

def on_device(
    branch_in, cotangent, weight_a, weight_x, conv_weight, conv_bias, bias_a, bias_x, rate
):
    inputs = branch_in[0]
    upstream = cotangent[0].astype(jnp.float32)
    length = inputs.shape[0]
    taps = conv_weight.shape[0]
    rows, cols = weight_a.shape
    dp_size = lax.axis_size("dp")
    ctx_size = lax.axis_size("ctx")
    packed = jnp.concatenate(
        [conv_weight, conv_bias[None], bias_a[None], bias_x[None], rate[None]], 0
    )
    width = ctx_size * cols
    joined = jnp.concatenate([weight_a, weight_x, packed], 0)
    by_ctx = gathered_by_doubling(joined, "ctx", bit_steps(ctx_size))
    by_ctx = by_ctx.transpose(1, 0, 2).reshape(joined.shape[0], width)
    params = by_ctx[2 * rows :]
    by_dp = gathered_by_doubling(by_ctx[: 2 * rows], "dp", bit_steps(dp_size)[::-1])
    full_a = by_dp[:, :rows].reshape(dp_size * rows, width)
    full_x = by_dp[:, rows:].reshape(dp_size * rows, width)
    head_width = dp_size * rows
    params = params.astype(jnp.float32)
    taps_f = params[:taps]
    cbias = params[taps]
    abias = params[taps + 1]
    xbias = params[taps + 2]
    rates = params[taps + 3]
    tail = passed_along(inputs[length - (taps - 1) :], "ctx", 1)
    padded = jnp.concatenate([tail, inputs], 0).astype(jnp.float32)
    conv = cbias
    for tap in range(taps):
        conv = conv + taps_f[tap] * padded[tap : tap + length]
    conv_b = conv.astype(jnp.bfloat16)
    conv_f = conv_b.astype(jnp.float32)
    recur_gate = jax.nn.sigmoid(mix_heads(conv_b, full_a) + abias)
    input_gate = jax.nn.sigmoid(mix_heads(conv_b, full_x) + xbias)
    log_decay = -8.0 * recur_gate * rates
    decay = jnp.exp(log_decay)
    one_minus = -jnp.expm1(2.0 * log_decay)
    multiplier = jnp.sqrt(jnp.maximum(one_minus, floor_value))
    drive = multiplier * input_gate * conv_f

    row_id = lax.broadcasted_iota(jnp.int32, (length, length), 0)
    col_id = lax.broadcasted_iota(jnp.int32, (length, length), 1)
    lower = (row_id >= col_id).astype(jnp.float32)
    upper = (row_id <= col_id).astype(jnp.float32)
    cum_log = jnp.dot(lower, log_decay, precision=exact)
    grow = jnp.exp(cum_log)
    shrink = jnp.exp(-cum_log)
    local_hidden = grow * jnp.dot(lower, shrink * drive, precision=exact)
    weighted_back = jnp.dot(upper, grow * upstream, precision=exact)
    local_back = shrink * weighted_back
    block_decay = grow[-1]
    state_in, back_in = block_prefix(block_decay, local_hidden[-1], weighted_back[0], "ctx")
    hidden = local_hidden + grow * state_in
    previous = jnp.concatenate([state_in[None], hidden[:-1]], 0)
    back = local_back + (block_decay * shrink) * back_in
    slope = jnp.where(one_minus > floor_value, 0.5 / multiplier, 0.0)
    d_mult = back * input_gate * conv_f
    d_log = back * previous * decay - 2.0 * decay * decay * d_mult * slope
    d_recur = (d_log * (-8.0 * rates) * recur_gate * (1.0 - recur_gate)).astype(jnp.bfloat16)
    d_input = (back * multiplier * conv_f * input_gate * (1.0 - input_gate)).astype(jnp.bfloat16)
    d_conv = (
        back * multiplier * input_gate + back_heads(d_recur, full_a) + back_heads(d_input, full_x)
    )
    following = passed_along(d_conv[: taps - 1], "ctx", -1)
    dpad = jnp.concatenate([d_conv, following], 0)
    grad_in = jnp.zeros((length, width), jnp.float32)
    for tap in range(taps):
        start = taps - 1 - tap
        grad_in = grad_in + taps_f[tap] * dpad[start : start + length]
    local_wgrad = grad_heads(conv_b, d_recur, head_width)
    local_rgrad = jnp.sum(d_log * (-8.0 * recur_gate), axis=0)
    by_row = local_wgrad.reshape(dp_size, rows * width)
    row_sum, rgrad = summed_apart(by_row, local_rgrad, "dp", digit_steps(dp_size))
    by_channel = row_sum.reshape(rows, ctx_size, cols).transpose(1, 0, 2)
    channel_sum, rgrad = summed_apart(
        by_channel.reshape(ctx_size, rows * cols), rgrad, "ctx", digit_steps(ctx_size)
    )
    wgrad = channel_sum.reshape(rows, cols)
    return (grad_in.astype(jnp.bfloat16)[None], wgrad, rgrad)


def solution(mesh):
    placed = (
        P("dp", "ctx", None),
        P("dp", "ctx", None),
        P("dp", "ctx"),
        P("dp", "ctx"),
        P(None, "ctx"),
        P("ctx"),
        P("ctx"),
        P("ctx"),
        P("ctx"),
    )
    return jax.shard_map(
        on_device,
        mesh=mesh,
        in_specs=placed,
        out_specs=(P("dp", "ctx", None), P("dp", "ctx"), P()),
        check_vma=False,
    )
```

```python
import jax
import jax.numpy as jnp
from jax import lax
from jax.sharding import PartitionSpec as P

floor_value = 2.5e-07
exact = lax.Precision.HIGHEST


def passed_along(array, axis, by):
    length = lax.axis_size(axis)
    pairs = [(i, i + by) for i in range(length) if 0 <= i + by < length]
    return lax.ppermute(array, axis, pairs)


def mix_heads(values, weights):
    tokens = values.shape[0]
    head_count, head_width, _ = weights.shape
    left = values.reshape(tokens, head_count, head_width)
    result = jnp.einsum("thk,hkj->thj", left, weights, preferred_element_type=jnp.float32)
    return result.reshape(tokens, head_count * head_width)


def back_heads(grads, weights):
    tokens = grads.shape[0]
    head_count, head_width, _ = weights.shape
    left = grads.reshape(tokens, head_count, head_width)
    result = jnp.einsum("thj,hkj->thk", left, weights, preferred_element_type=jnp.float32)
    return result.reshape(tokens, head_count * head_width)


def grad_heads(values, grads, head_width):
    tokens = values.shape[0]
    head_count = values.shape[1] // head_width
    left = values.reshape(tokens, head_count, head_width)
    right = grads.reshape(tokens, head_count, head_width)
    result = jnp.einsum("thk,thj->khj", left, right, preferred_element_type=jnp.float32)
    return result.reshape(head_width, head_count * head_width)


def compose(own, received):
    return (own[0] * received[0], own[0] * received[1] + own[1])


def block_prefix(decay_all, forward_all, backward_all, axis):
    span = lax.axis_size(axis)
    me = lax.axis_index(axis)
    ones = jnp.ones_like(decay_all)
    zeros = jnp.zeros_like(decay_all)
    group = (decay_all, forward_all, backward_all)
    before = (ones, zeros)
    after = (ones, zeros)
    stride = 1
    while stride < span:
        got = exchanged(jnp.stack(group), axis, stride)
        other = (got[0], got[1], got[2])
        right_half = (me // stride) % 2 == 1
        mixed_before = compose(before, (other[0], other[1]))
        mixed_after = compose(after, (other[0], other[2]))
        before = tuple(jnp.where(right_half, n, o) for n, o in zip(mixed_before, before))
        after = tuple(jnp.where(right_half, o, n) for n, o in zip(mixed_after, after))
        forward_total = jnp.where(
            right_half, group[0] * other[1] + group[1], other[0] * group[1] + other[1]
        )
        backward_total = jnp.where(
            right_half, other[0] * group[2] + other[2], group[0] * other[2] + group[2]
        )
        group = (group[0] * other[0], forward_total, backward_total)
        stride *= 2
    return before[1], after[1]

def bit_steps(length):
    return [[stride] for step in digit_steps(length) for stride in step]


def digit_steps(length):
    bits = []
    stride = 1
    while stride < length:
        bits.append(stride)
        stride *= 2
    return [bits[i : i + 2] for i in range(0, len(bits), 2)]


def exchanged(array, axis, mask):
    length = lax.axis_size(axis)
    return lax.ppermute(array, axis, [(i, i ^ mask) for i in range(length)])


def patterns(step):
    masks = [0]
    for stride in step:
        masks = masks + [m + stride for m in masks]
    return masks


def digit_of(me, step):
    value = jnp.int32(0)
    for place, stride in enumerate(step):
        value = value + ((me // stride) % 2) * (2**place)
    return value


def mask_of(pattern_index, step):
    mask = 0
    for place, stride in enumerate(step):
        if (pattern_index >> place) & 1:
            mask += stride
    return mask


def gathered_by_doubling(piece, axis, steps):
    length = lax.axis_size(axis)
    me = lax.axis_index(axis)
    held = piece
    done = 0
    order = []
    for step in steps:
        size = 2 ** len(step)
        mine = digit_of(me, step)
        sources = [held] + [exchanged(held, axis, mask_of(p, step)) for p in range(1, size)]
        pool = jnp.stack(sources, 0)
        slots = [
            lax.dynamic_index_in_dim(pool, jnp.bitwise_xor(mine, v), 0, keepdims=False)
            for v in range(size)
        ]
        held = jnp.stack(slots, done)
        held = held.reshape(held.shape[:done] + (2,) * len(step) + held.shape[done + 1 :])
        order = order + step[::-1]
        done += len(step)
    rank = sorted(range(done), key=lambda j: -order[j])
    held = held.transpose(rank + list(range(done, held.ndim)))
    return held.reshape((length,) + piece.shape)


def summed_by_halving(blocks, axis, steps):
    length = lax.axis_size(axis)
    me = lax.axis_index(axis)
    bits = []
    stride = length // 2
    while stride >= 1:
        bits.append(stride)
        stride //= 2
    held = blocks
    for step in steps:
        size = 2 ** len(step)
        mine = digit_of(me, step)
        rest = [b for b in bits if b not in step]
        front = held.reshape((2,) * len(bits) + blocks.shape[1:]) if bits else held
        lead = [bits.index(b) for b in step[::-1]] + [bits.index(b) for b in rest]
        front = front.transpose(lead + list(range(len(bits), front.ndim)))
        front = front.reshape((size,) + (2 ** len(rest),) + blocks.shape[1:])
        total = lax.dynamic_index_in_dim(front, mine, 0, keepdims=False)
        for p in range(1, size):
            give = lax.dynamic_index_in_dim(front, jnp.bitwise_xor(mine, p), 0, keepdims=False)
            total = total + exchanged(give, axis, mask_of(p, step))
        held = total
        bits = rest
    return held[0]

def summed_apart(parts, shared, axis, steps):
    count, height, size = parts.shape
    shared_rows = shared.reshape(height, -1)
    stacked = jnp.concatenate(
        [parts, jnp.broadcast_to(shared_rows[None], (count,) + shared_rows.shape)], 2
    )
    mine = summed_by_halving(stacked, axis, steps)
    return mine[:, :size], mine[:, size:].reshape(-1)

def on_device(
    branch_in, cotangent, weight_a, weight_x, conv_weight, conv_bias, bias_a, bias_x, rate
):
    inputs = branch_in[0]
    upstream = cotangent[0].astype(jnp.float32)
    length = inputs.shape[0]
    taps = conv_weight.shape[0]
    rows, cols = weight_a.shape
    dp_size = lax.axis_size("dp")
    ctx_size = lax.axis_size("ctx")
    packed = jnp.concatenate(
        [conv_weight, conv_bias[None], bias_a[None], bias_x[None], rate[None]], 0
    )
    width = ctx_size * cols
    head_width = dp_size * rows
    joined = jnp.concatenate([weight_a, weight_x, packed], 0)
    by_ctx = gathered_by_doubling(joined, "ctx", bit_steps(ctx_size))
    by_ctx = by_ctx.transpose(1, 0, 2).reshape(joined.shape[0], width)
    params = by_ctx[2 * rows :]
    heads = by_ctx[: 2 * rows].reshape(2 * rows, -1, head_width).transpose(1, 0, 2)
    by_dp = gathered_by_doubling(heads, "dp", bit_steps(dp_size)[::-1])
    head_count = heads.shape[0]

    def head_major(part):
        return part.transpose(1, 0, 2, 3).reshape(head_count, dp_size * rows, head_width)

    full_a = head_major(by_dp[:, :, :rows])
    full_x = head_major(by_dp[:, :, rows:])
    params = params.astype(jnp.float32)
    taps_f = params[:taps]
    cbias = params[taps]
    abias = params[taps + 1]
    xbias = params[taps + 2]
    rates = params[taps + 3]
    tail = passed_along(inputs[length - (taps - 1) :], "ctx", 1)
    padded = jnp.concatenate([tail, inputs], 0).astype(jnp.float32)
    conv = cbias
    for tap in range(taps):
        conv = conv + taps_f[tap] * padded[tap : tap + length]
    conv_b = conv.astype(jnp.bfloat16)
    conv_f = conv_b.astype(jnp.float32)
    recur_gate = jax.nn.sigmoid(mix_heads(conv_b, full_a) + abias)
    input_gate = jax.nn.sigmoid(mix_heads(conv_b, full_x) + xbias)
    log_decay = -8.0 * recur_gate * rates
    decay = jnp.exp(log_decay)
    one_minus = -jnp.expm1(2.0 * log_decay)
    multiplier = jnp.sqrt(jnp.maximum(one_minus, floor_value))
    drive = multiplier * input_gate * conv_f

    row_id = lax.broadcasted_iota(jnp.int32, (length, length), 0)
    col_id = lax.broadcasted_iota(jnp.int32, (length, length), 1)
    lower = (row_id >= col_id).astype(jnp.float32)
    upper = (row_id <= col_id).astype(jnp.float32)
    cum_log = jnp.dot(lower, log_decay, precision=exact)
    grow = jnp.exp(cum_log)
    shrink = jnp.exp(-cum_log)
    local_hidden = grow * jnp.dot(lower, shrink * drive, precision=exact)
    weighted_back = jnp.dot(upper, grow * upstream, precision=exact)
    local_back = shrink * weighted_back
    block_decay = grow[-1]
    state_in, back_in = block_prefix(block_decay, local_hidden[-1], weighted_back[0], "ctx")
    hidden = local_hidden + grow * state_in
    previous = jnp.concatenate([state_in[None], hidden[:-1]], 0)
    back = local_back + (block_decay * shrink) * back_in
    slope = jnp.where(one_minus > floor_value, 0.5 / multiplier, 0.0)
    d_mult = back * input_gate * conv_f
    d_log = back * previous * decay - 2.0 * decay * decay * d_mult * slope
    d_recur = (d_log * (-8.0 * rates) * recur_gate * (1.0 - recur_gate)).astype(jnp.bfloat16)
    d_input = (back * multiplier * conv_f * input_gate * (1.0 - input_gate)).astype(jnp.bfloat16)
    d_conv = (
        back * multiplier * input_gate + back_heads(d_recur, full_a) + back_heads(d_input, full_x)
    )
    following = passed_along(d_conv[: taps - 1], "ctx", -1)
    dpad = jnp.concatenate([d_conv, following], 0)
    grad_in = jnp.zeros((length, width), jnp.float32)
    for tap in range(taps):
        start = taps - 1 - tap
        grad_in = grad_in + taps_f[tap] * dpad[start : start + length]
    local_wgrad = grad_heads(conv_b, d_recur, head_width)
    local_rgrad = jnp.sum(d_log * (-8.0 * recur_gate), axis=0)
    by_row = local_wgrad.reshape(dp_size, rows, width)
    row_sum, rgrad = summed_apart(by_row, local_rgrad, "dp", digit_steps(dp_size))
    by_channel = row_sum.reshape(rows, ctx_size, cols).transpose(1, 0, 2)
    wgrad, rgrad = summed_apart(by_channel, rgrad, "ctx", digit_steps(ctx_size))
    return (grad_in.astype(jnp.bfloat16)[None], wgrad, rgrad)


def solution(mesh):
    placed = (
        P("dp", "ctx", None),
        P("dp", "ctx", None),
        P("dp", "ctx"),
        P("dp", "ctx"),
        P(None, "ctx"),
        P("ctx"),
        P("ctx"),
        P("ctx"),
        P("ctx"),
    )
    return jax.shard_map(
        on_device,
        mesh=mesh,
        in_specs=placed,
        out_specs=(P("dp", "ctx", None), P("dp", "ctx"), P()),
        check_vma=False,
    )
```

```python
import jax
import jax.numpy as jnp
from jax import lax
from jax.sharding import PartitionSpec as P

floor_value = 2.5e-07
exact = lax.Precision.HIGHEST


def passed_along(array, axis, by):
    length = lax.axis_size(axis)
    pairs = [(i, i + by) for i in range(length) if 0 <= i + by < length]
    return lax.ppermute(array, axis, pairs)


def mix_heads(values, weights):
    tokens = values.shape[0]
    head_count, head_width, _ = weights.shape
    left = values.reshape(tokens, head_count, head_width)
    result = jnp.einsum("thk,hkj->thj", left, weights, preferred_element_type=jnp.float32)
    return result.reshape(tokens, head_count * head_width)


def back_heads(grads, weights):
    tokens = grads.shape[0]
    head_count, head_width, _ = weights.shape
    left = grads.reshape(tokens, head_count, head_width)
    result = jnp.einsum("thj,hkj->thk", left, weights, preferred_element_type=jnp.float32)
    return result.reshape(tokens, head_count * head_width)


def grad_heads(values, grads, head_width):
    tokens = values.shape[0]
    head_count = values.shape[1] // head_width
    left = values.reshape(tokens, head_count, head_width)
    right = grads.reshape(tokens, head_count, head_width)
    result = jnp.einsum("thk,thj->khj", left, right, preferred_element_type=jnp.float32)
    return result.reshape(head_width, head_count * head_width)


def compose(own, received):
    return (own[0] * received[0], own[0] * received[1] + own[1])


def block_prefix(decay_all, forward_all, backward_all, axis):
    span = lax.axis_size(axis)
    me = lax.axis_index(axis)
    ones = jnp.ones_like(decay_all)
    zeros = jnp.zeros_like(decay_all)
    group = (decay_all, forward_all, backward_all)
    before = (ones, zeros)
    after = (ones, zeros)
    stride = 1
    while stride < span:
        got = exchanged(jnp.stack(group), axis, stride)
        other = (got[0], got[1], got[2])
        right_half = (me // stride) % 2 == 1
        mixed_before = compose(before, (other[0], other[1]))
        mixed_after = compose(after, (other[0], other[2]))
        before = tuple(jnp.where(right_half, n, o) for n, o in zip(mixed_before, before))
        after = tuple(jnp.where(right_half, o, n) for n, o in zip(mixed_after, after))
        forward_total = jnp.where(
            right_half, group[0] * other[1] + group[1], other[0] * group[1] + other[1]
        )
        backward_total = jnp.where(
            right_half, other[0] * group[2] + other[2], group[0] * other[2] + group[2]
        )
        group = (group[0] * other[0], forward_total, backward_total)
        stride *= 2
    return before[1], after[1]

def core_first_steps(length):
    bits = [stride for step in digit_steps(length) for stride in step]
    return [bits[:1]] + [bits[i : i + 2] for i in range(1, len(bits), 2)]


def bit_steps(length):
    return [[stride] for step in digit_steps(length) for stride in step]


def digit_steps(length):
    bits = []
    stride = 1
    while stride < length:
        bits.append(stride)
        stride *= 2
    return [bits[i : i + 2] for i in range(0, len(bits), 2)]


def exchanged(array, axis, mask):
    length = lax.axis_size(axis)
    return lax.ppermute(array, axis, [(i, i ^ mask) for i in range(length)])


def patterns(step):
    masks = [0]
    for stride in step:
        masks = masks + [m + stride for m in masks]
    return masks


def digit_of(me, step):
    value = jnp.int32(0)
    for place, stride in enumerate(step):
        value = value + ((me // stride) % 2) * (2**place)
    return value


def mask_of(pattern_index, step):
    mask = 0
    for place, stride in enumerate(step):
        if (pattern_index >> place) & 1:
            mask += stride
    return mask


def gathered_by_doubling(piece, axis, steps):
    length = lax.axis_size(axis)
    me = lax.axis_index(axis)
    held = piece
    done = 0
    order = []
    for step in steps:
        size = 2 ** len(step)
        mine = digit_of(me, step)
        sources = [held] + [exchanged(held, axis, mask_of(p, step)) for p in range(1, size)]
        pool = jnp.stack(sources, 0)
        slots = [
            lax.dynamic_index_in_dim(pool, jnp.bitwise_xor(mine, v), 0, keepdims=False)
            for v in range(size)
        ]
        held = jnp.stack(slots, done)
        held = held.reshape(held.shape[:done] + (2,) * len(step) + held.shape[done + 1 :])
        order = order + step[::-1]
        done += len(step)
    rank = sorted(range(done), key=lambda j: -order[j])
    held = held.transpose(rank + list(range(done, held.ndim)))
    return held.reshape((length,) + piece.shape)


def summed_by_halving(blocks, axis, steps):
    length = lax.axis_size(axis)
    me = lax.axis_index(axis)
    bits = []
    stride = length // 2
    while stride >= 1:
        bits.append(stride)
        stride //= 2
    held = blocks
    for step in steps:
        size = 2 ** len(step)
        mine = digit_of(me, step)
        rest = [b for b in bits if b not in step]
        front = held.reshape((2,) * len(bits) + blocks.shape[1:]) if bits else held
        lead = [bits.index(b) for b in step[::-1]] + [bits.index(b) for b in rest]
        front = front.transpose(lead + list(range(len(bits), front.ndim)))
        front = front.reshape((size,) + (2 ** len(rest),) + blocks.shape[1:])
        total = lax.dynamic_index_in_dim(front, mine, 0, keepdims=False)
        for p in range(1, size):
            give = lax.dynamic_index_in_dim(front, jnp.bitwise_xor(mine, p), 0, keepdims=False)
            total = total + exchanged(give, axis, mask_of(p, step))
        held = total
        bits = rest
    return held[0]

def summed_apart(parts, shared, axis, steps):
    count, height, size = parts.shape
    shared_rows = shared.reshape(height, -1)
    stacked = jnp.concatenate(
        [parts, jnp.broadcast_to(shared_rows[None], (count,) + shared_rows.shape)], 2
    )
    mine = summed_by_halving(stacked, axis, steps)
    return mine[:, :size], mine[:, size:].reshape(-1)

def on_device(
    branch_in, cotangent, weight_a, weight_x, conv_weight, conv_bias, bias_a, bias_x, rate
):
    inputs = branch_in[0]
    upstream = cotangent[0].astype(jnp.float32)
    length = inputs.shape[0]
    taps = conv_weight.shape[0]
    rows, cols = weight_a.shape
    dp_size = lax.axis_size("dp")
    ctx_size = lax.axis_size("ctx")
    packed = jnp.concatenate(
        [conv_weight, conv_bias[None], bias_a[None], bias_x[None], rate[None]], 0
    )
    width = ctx_size * cols
    head_width = dp_size * rows
    joined = jnp.concatenate([weight_a, weight_x, packed], 0)
    by_ctx = gathered_by_doubling(joined, "ctx", bit_steps(ctx_size))
    by_ctx = by_ctx.transpose(1, 0, 2).reshape(joined.shape[0], width)
    params = by_ctx[2 * rows :]
    heads = by_ctx[: 2 * rows].reshape(2 * rows, -1, head_width).transpose(1, 0, 2)
    by_dp = gathered_by_doubling(heads, "dp", bit_steps(dp_size)[::-1])
    head_count = heads.shape[0]

    def head_major(part):
        return part.transpose(1, 0, 2, 3).reshape(head_count, dp_size * rows, head_width)

    full_a = head_major(by_dp[:, :, :rows])
    full_x = head_major(by_dp[:, :, rows:])
    params = params.astype(jnp.float32)
    taps_f = params[:taps]
    cbias = params[taps]
    abias = params[taps + 1]
    xbias = params[taps + 2]
    rates = params[taps + 3]
    tail = passed_along(inputs[length - (taps - 1) :], "ctx", 1)
    padded = jnp.concatenate([tail, inputs], 0).astype(jnp.float32)
    conv = cbias
    for tap in range(taps):
        conv = conv + taps_f[tap] * padded[tap : tap + length]
    conv_b = conv.astype(jnp.bfloat16)
    conv_f = conv_b.astype(jnp.float32)
    recur_gate = jax.nn.sigmoid(mix_heads(conv_b, full_a) + abias)
    input_gate = jax.nn.sigmoid(mix_heads(conv_b, full_x) + xbias)
    log_decay = -8.0 * recur_gate * rates
    decay = jnp.exp(log_decay)
    one_minus = -jnp.expm1(2.0 * log_decay)
    multiplier = jnp.sqrt(jnp.maximum(one_minus, floor_value))
    drive = multiplier * input_gate * conv_f

    row_id = lax.broadcasted_iota(jnp.int32, (length, length), 0)
    col_id = lax.broadcasted_iota(jnp.int32, (length, length), 1)
    lower = (row_id >= col_id).astype(jnp.float32)
    upper = (row_id <= col_id).astype(jnp.float32)
    cum_log = jnp.dot(lower, log_decay, precision=exact)
    grow = jnp.exp(cum_log)
    shrink = jnp.exp(-cum_log)
    local_hidden = grow * jnp.dot(lower, shrink * drive, precision=exact)
    weighted_back = jnp.dot(upper, grow * upstream, precision=exact)
    local_back = shrink * weighted_back
    block_decay = grow[-1]
    state_in, back_in = block_prefix(block_decay, local_hidden[-1], weighted_back[0], "ctx")
    hidden = local_hidden + grow * state_in
    previous = jnp.concatenate([state_in[None], hidden[:-1]], 0)
    back = local_back + (block_decay * shrink) * back_in
    slope = jnp.where(one_minus > floor_value, 0.5 / multiplier, 0.0)
    d_mult = back * input_gate * conv_f
    d_log = back * previous * decay - 2.0 * decay * decay * d_mult * slope
    d_recur = (d_log * (-8.0 * rates) * recur_gate * (1.0 - recur_gate)).astype(jnp.bfloat16)
    d_input = (back * multiplier * conv_f * input_gate * (1.0 - input_gate)).astype(jnp.bfloat16)
    d_conv = (
        back * multiplier * input_gate + back_heads(d_recur, full_a) + back_heads(d_input, full_x)
    )
    following = passed_along(d_conv[: taps - 1], "ctx", -1)
    dpad = jnp.concatenate([d_conv, following], 0)
    grad_in = jnp.zeros((length, width), jnp.float32)
    for tap in range(taps):
        start = taps - 1 - tap
        grad_in = grad_in + taps_f[tap] * dpad[start : start + length]
    local_wgrad = grad_heads(conv_b, d_recur, head_width)
    local_rgrad = jnp.sum(d_log * (-8.0 * recur_gate), axis=0)
    by_row = local_wgrad.reshape(dp_size, rows, width)
    row_sum, rgrad = summed_apart(by_row, local_rgrad, "dp", core_first_steps(dp_size))
    by_channel = row_sum.reshape(rows, ctx_size, cols).transpose(1, 0, 2)
    wgrad, rgrad = summed_apart(by_channel, rgrad, "ctx", digit_steps(ctx_size))
    return (grad_in.astype(jnp.bfloat16)[None], wgrad, rgrad)


def solution(mesh):
    placed = (
        P("dp", "ctx", None),
        P("dp", "ctx", None),
        P("dp", "ctx"),
        P("dp", "ctx"),
        P(None, "ctx"),
        P("ctx"),
        P("ctx"),
        P("ctx"),
        P("ctx"),
    )
    return jax.shard_map(
        on_device,
        mesh=mesh,
        in_specs=placed,
        out_specs=(P("dp", "ctx", None), P("dp", "ctx"), P()),
        check_vma=False,
    )
```

```python
import jax
import jax.numpy as jnp
from jax import lax
from jax.sharding import PartitionSpec as P

floor_value = 2.5e-07
exact = lax.Precision.HIGHEST


def passed_along(array, axis, by):
    length = lax.axis_size(axis)
    pairs = [(i, i + by) for i in range(length) if 0 <= i + by < length]
    return lax.ppermute(array, axis, pairs)


def mix_heads(values, weights):
    tokens = values.shape[0]
    head_count, head_width, _ = weights.shape
    left = values.reshape(tokens, head_count, head_width)
    result = jnp.einsum("thk,hkj->thj", left, weights, preferred_element_type=jnp.float32)
    return result.reshape(tokens, head_count * head_width)


def back_heads(grads, weights):
    tokens = grads.shape[0]
    head_count, head_width, _ = weights.shape
    left = grads.reshape(tokens, head_count, head_width)
    result = jnp.einsum("thj,hkj->thk", left, weights, preferred_element_type=jnp.float32)
    return result.reshape(tokens, head_count * head_width)


def grad_heads(values, grads, head_width):
    tokens = values.shape[0]
    head_count = values.shape[1] // head_width
    left = values.reshape(tokens, head_count, head_width)
    right = grads.reshape(tokens, head_count, head_width)
    result = jnp.einsum("thk,thj->khj", left, right, preferred_element_type=jnp.float32)
    return result.reshape(head_width, head_count * head_width)


def compose(own, received):
    return (own[0] * received[0], own[0] * received[1] + own[1])


def block_prefix(decay_all, forward_all, backward_all, axis):
    span = lax.axis_size(axis)
    me = lax.axis_index(axis)
    ones = jnp.ones_like(decay_all)
    zeros = jnp.zeros_like(decay_all)
    group = (decay_all, forward_all, backward_all)
    before = (ones, zeros)
    after = (ones, zeros)
    stride = 1
    while stride < span:
        got = exchanged(jnp.stack(group), axis, stride)
        other = (got[0], got[1], got[2])
        right_half = (me // stride) % 2 == 1
        mixed_before = compose(before, (other[0], other[1]))
        mixed_after = compose(after, (other[0], other[2]))
        before = tuple(jnp.where(right_half, n, o) for n, o in zip(mixed_before, before))
        after = tuple(jnp.where(right_half, o, n) for n, o in zip(mixed_after, after))
        forward_total = jnp.where(
            right_half, group[0] * other[1] + group[1], other[0] * group[1] + other[1]
        )
        backward_total = jnp.where(
            right_half, other[0] * group[2] + other[2], group[0] * other[2] + group[2]
        )
        group = (group[0] * other[0], forward_total, backward_total)
        stride *= 2
    return before[1], after[1]

def core_first_steps(length):
    bits = [stride for step in digit_steps(length) for stride in step]
    return [bits[:1]] + [bits[i : i + 2] for i in range(1, len(bits), 2)]


def spread_steps(length, first):
    bits = [stride for step in digit_steps(length) for stride in step]
    head, rest = bits[:first], bits[first:]
    half = (len(rest) + 1) // 2
    low, high = rest[:half], rest[half:]
    steps = [[b] for b in head]
    for i, b in enumerate(low):
        steps.append([b, high[i]] if i < len(high) else [b])
    return steps


def bit_steps(length):
    return [[stride] for step in digit_steps(length) for stride in step]


def digit_steps(length):
    bits = []
    stride = 1
    while stride < length:
        bits.append(stride)
        stride *= 2
    return [bits[i : i + 2] for i in range(0, len(bits), 2)]


def exchanged(array, axis, mask):
    length = lax.axis_size(axis)
    return lax.ppermute(array, axis, [(i, i ^ mask) for i in range(length)])


def patterns(step):
    masks = [0]
    for stride in step:
        masks = masks + [m + stride for m in masks]
    return masks


def digit_of(me, step):
    value = jnp.int32(0)
    for place, stride in enumerate(step):
        value = value + ((me // stride) % 2) * (2**place)
    return value


def mask_of(pattern_index, step):
    mask = 0
    for place, stride in enumerate(step):
        if (pattern_index >> place) & 1:
            mask += stride
    return mask


def gathered_by_doubling(piece, axis, steps):
    length = lax.axis_size(axis)
    me = lax.axis_index(axis)
    held = piece
    done = 0
    order = []
    for step in steps:
        size = 2 ** len(step)
        mine = digit_of(me, step)
        sources = [held] + [exchanged(held, axis, mask_of(p, step)) for p in range(1, size)]
        pool = jnp.stack(sources, 0)
        slots = [
            lax.dynamic_index_in_dim(pool, jnp.bitwise_xor(mine, v), 0, keepdims=False)
            for v in range(size)
        ]
        held = jnp.stack(slots, done)
        held = held.reshape(held.shape[:done] + (2,) * len(step) + held.shape[done + 1 :])
        order = order + step[::-1]
        done += len(step)
    rank = sorted(range(done), key=lambda j: -order[j])
    held = held.transpose(rank + list(range(done, held.ndim)))
    return held.reshape((length,) + piece.shape)


def summed_by_halving(blocks, axis, steps):
    length = lax.axis_size(axis)
    me = lax.axis_index(axis)
    bits = []
    stride = length // 2
    while stride >= 1:
        bits.append(stride)
        stride //= 2
    held = blocks
    for step in steps:
        size = 2 ** len(step)
        mine = digit_of(me, step)
        rest = [b for b in bits if b not in step]
        front = held.reshape((2,) * len(bits) + blocks.shape[1:]) if bits else held
        lead = [bits.index(b) for b in step[::-1]] + [bits.index(b) for b in rest]
        front = front.transpose(lead + list(range(len(bits), front.ndim)))
        front = front.reshape((size,) + (2 ** len(rest),) + blocks.shape[1:])
        total = lax.dynamic_index_in_dim(front, mine, 0, keepdims=False)
        for p in range(1, size):
            give = lax.dynamic_index_in_dim(front, jnp.bitwise_xor(mine, p), 0, keepdims=False)
            total = total + exchanged(give, axis, mask_of(p, step))
        held = total
        bits = rest
    return held[0]

def summed_apart(parts, shared, axis, steps):
    count, height, size = parts.shape
    shared_rows = shared.reshape(height, -1)
    stacked = jnp.concatenate(
        [parts, jnp.broadcast_to(shared_rows[None], (count,) + shared_rows.shape)], 2
    )
    mine = summed_by_halving(stacked, axis, steps)
    return mine[:, :size], mine[:, size:].reshape(-1)

def on_device(
    branch_in, cotangent, weight_a, weight_x, conv_weight, conv_bias, bias_a, bias_x, rate
):
    inputs = branch_in[0]
    upstream = cotangent[0].astype(jnp.float32)
    length = inputs.shape[0]
    taps = conv_weight.shape[0]
    rows, cols = weight_a.shape
    dp_size = lax.axis_size("dp")
    ctx_size = lax.axis_size("ctx")
    packed = jnp.concatenate(
        [conv_weight, conv_bias[None], bias_a[None], bias_x[None], rate[None]], 0
    )
    width = ctx_size * cols
    head_width = dp_size * rows
    joined = jnp.concatenate([weight_a, weight_x, packed], 0)
    by_ctx = gathered_by_doubling(joined, "ctx", bit_steps(ctx_size))
    by_ctx = by_ctx.transpose(1, 0, 2).reshape(joined.shape[0], width)
    params = by_ctx[2 * rows :]
    heads = by_ctx[: 2 * rows].reshape(2 * rows, -1, head_width).transpose(1, 0, 2)
    by_dp = gathered_by_doubling(heads, "dp", bit_steps(dp_size)[::-1])
    head_count = heads.shape[0]

    def head_major(part):
        return part.transpose(1, 0, 2, 3).reshape(head_count, dp_size * rows, head_width)

    full_a = head_major(by_dp[:, :, :rows])
    full_x = head_major(by_dp[:, :, rows:])
    params = params.astype(jnp.float32)
    taps_f = params[:taps]
    cbias = params[taps]
    abias = params[taps + 1]
    xbias = params[taps + 2]
    rates = params[taps + 3]
    tail = passed_along(inputs[length - (taps - 1) :], "ctx", 1)
    padded = jnp.concatenate([tail, inputs], 0).astype(jnp.float32)
    conv = cbias
    for tap in range(taps):
        conv = conv + taps_f[tap] * padded[tap : tap + length]
    conv_b = conv.astype(jnp.bfloat16)
    conv_f = conv_b.astype(jnp.float32)
    recur_gate = jax.nn.sigmoid(mix_heads(conv_b, full_a) + abias)
    input_gate = jax.nn.sigmoid(mix_heads(conv_b, full_x) + xbias)
    log_decay = -8.0 * recur_gate * rates
    decay = jnp.exp(log_decay)
    one_minus = -jnp.expm1(2.0 * log_decay)
    multiplier = jnp.sqrt(jnp.maximum(one_minus, floor_value))
    drive = multiplier * input_gate * conv_f

    row_id = lax.broadcasted_iota(jnp.int32, (length, length), 0)
    col_id = lax.broadcasted_iota(jnp.int32, (length, length), 1)
    lower = (row_id >= col_id).astype(jnp.float32)
    upper = (row_id <= col_id).astype(jnp.float32)
    cum_log = jnp.dot(lower, log_decay, precision=exact)
    grow = jnp.exp(cum_log)
    shrink = jnp.exp(-cum_log)
    local_hidden = grow * jnp.dot(lower, shrink * drive, precision=exact)
    weighted_back = jnp.dot(upper, grow * upstream, precision=exact)
    local_back = shrink * weighted_back
    block_decay = grow[-1]
    state_in, back_in = block_prefix(block_decay, local_hidden[-1], weighted_back[0], "ctx")
    hidden = local_hidden + grow * state_in
    previous = jnp.concatenate([state_in[None], hidden[:-1]], 0)
    back = local_back + (block_decay * shrink) * back_in
    slope = jnp.where(one_minus > floor_value, 0.5 / multiplier, 0.0)
    d_mult = back * input_gate * conv_f
    d_log = back * previous * decay - 2.0 * decay * decay * d_mult * slope
    d_recur = (d_log * (-8.0 * rates) * recur_gate * (1.0 - recur_gate)).astype(jnp.bfloat16)
    d_input = (back * multiplier * conv_f * input_gate * (1.0 - input_gate)).astype(jnp.bfloat16)
    d_conv = (
        back * multiplier * input_gate + back_heads(d_recur, full_a) + back_heads(d_input, full_x)
    )
    following = passed_along(d_conv[: taps - 1], "ctx", -1)
    dpad = jnp.concatenate([d_conv, following], 0)
    grad_in = jnp.zeros((length, width), jnp.float32)
    for tap in range(taps):
        start = taps - 1 - tap
        grad_in = grad_in + taps_f[tap] * dpad[start : start + length]
    local_wgrad = grad_heads(conv_b, d_recur, head_width)
    local_rgrad = jnp.sum(d_log * (-8.0 * recur_gate), axis=0)
    by_row = local_wgrad.reshape(dp_size, rows, width)
    row_sum, rgrad = summed_apart(by_row, local_rgrad, "dp", spread_steps(dp_size, 1))
    by_channel = row_sum.reshape(rows, ctx_size, cols).transpose(1, 0, 2)
    wgrad, rgrad = summed_apart(by_channel, rgrad, "ctx", spread_steps(ctx_size, 0))
    return (grad_in.astype(jnp.bfloat16)[None], wgrad, rgrad)


def solution(mesh):
    placed = (
        P("dp", "ctx", None),
        P("dp", "ctx", None),
        P("dp", "ctx"),
        P("dp", "ctx"),
        P(None, "ctx"),
        P("ctx"),
        P("ctx"),
        P("ctx"),
        P("ctx"),
    )
    return jax.shard_map(
        on_device,
        mesh=mesh,
        in_specs=placed,
        out_specs=(P("dp", "ctx", None), P("dp", "ctx"), P()),
        check_vma=False,
    )
```

```python
import jax
import jax.numpy as jnp
from jax import lax
from jax.sharding import PartitionSpec as P

floor_value = 2.5e-07
exact = lax.Precision.HIGHEST


def passed_along(array, axis, by):
    length = lax.axis_size(axis)
    pairs = [(i, i + by) for i in range(length) if 0 <= i + by < length]
    return lax.ppermute(array, axis, pairs)


def mix_heads(values, weights):
    tokens = values.shape[0]
    head_count, head_width, _ = weights.shape
    left = values.reshape(tokens, head_count, head_width)
    result = jnp.einsum("thk,hkj->thj", left, weights, preferred_element_type=jnp.float32)
    return result.reshape(tokens, head_count * head_width)


def back_heads(grads, weights):
    tokens = grads.shape[0]
    head_count, head_width, _ = weights.shape
    left = grads.reshape(tokens, head_count, head_width)
    result = jnp.einsum("thj,hkj->thk", left, weights, preferred_element_type=jnp.float32)
    return result.reshape(tokens, head_count * head_width)


def grad_heads(values, grads, head_width):
    tokens = values.shape[0]
    head_count = values.shape[1] // head_width
    left = values.reshape(tokens, head_count, head_width)
    right = grads.reshape(tokens, head_count, head_width)
    result = jnp.einsum("thk,thj->khj", left, right, preferred_element_type=jnp.float32)
    return result.reshape(head_width, head_count * head_width)


def compose(own, received):
    return (own[0] * received[0], own[0] * received[1] + own[1])


def block_prefix(decay_all, forward_all, backward_all, axis):
    span = lax.axis_size(axis)
    me = lax.axis_index(axis)
    ones = jnp.ones_like(decay_all)
    zeros = jnp.zeros_like(decay_all)
    group = (decay_all, forward_all, backward_all)
    before = (ones, zeros)
    after = (ones, zeros)
    stride = 1
    while stride < span:
        got = exchanged(jnp.stack(group), axis, stride)
        other = (got[0], got[1], got[2])
        right_half = (me // stride) % 2 == 1
        mixed_before = compose(before, (other[0], other[1]))
        mixed_after = compose(after, (other[0], other[2]))
        before = tuple(jnp.where(right_half, n, o) for n, o in zip(mixed_before, before))
        after = tuple(jnp.where(right_half, o, n) for n, o in zip(mixed_after, after))
        forward_total = jnp.where(
            right_half, group[0] * other[1] + group[1], other[0] * group[1] + other[1]
        )
        backward_total = jnp.where(
            right_half, other[0] * group[2] + other[2], group[0] * other[2] + group[2]
        )
        group = (group[0] * other[0], forward_total, backward_total)
        stride *= 2
    return before[1], after[1]

def core_first_steps(length):
    bits = [stride for step in digit_steps(length) for stride in step]
    return [bits[:1]] + [bits[i : i + 2] for i in range(1, len(bits), 2)]


def spread_steps(length, first):
    bits = [stride for step in digit_steps(length) for stride in step]
    head, rest = bits[:first], bits[first:]
    half = (len(rest) + 1) // 2
    low, high = rest[:half], rest[half:]
    steps = [[b] for b in head]
    for i, b in enumerate(low):
        steps.append([b, high[i]] if i < len(high) else [b])
    return steps


def near_last(length):
    single = [[b] for b in [stride for step in spread_steps(length, 1) for stride in step]]
    return single[::-1]


def bit_steps(length):
    return [[stride] for step in digit_steps(length) for stride in step]


def digit_steps(length):
    bits = []
    stride = 1
    while stride < length:
        bits.append(stride)
        stride *= 2
    return [bits[i : i + 2] for i in range(0, len(bits), 2)]


def exchanged(array, axis, mask):
    length = lax.axis_size(axis)
    return lax.ppermute(array, axis, [(i, i ^ mask) for i in range(length)])


def patterns(step):
    masks = [0]
    for stride in step:
        masks = masks + [m + stride for m in masks]
    return masks


def digit_of(me, step):
    value = jnp.int32(0)
    for place, stride in enumerate(step):
        value = value + ((me // stride) % 2) * (2**place)
    return value


def mask_of(pattern_index, step):
    mask = 0
    for place, stride in enumerate(step):
        if (pattern_index >> place) & 1:
            mask += stride
    return mask


def gathered_by_doubling(piece, axis, steps):
    length = lax.axis_size(axis)
    me = lax.axis_index(axis)
    held = piece
    done = 0
    order = []
    for step in steps:
        size = 2 ** len(step)
        mine = digit_of(me, step)
        sources = [held] + [exchanged(held, axis, mask_of(p, step)) for p in range(1, size)]
        pool = jnp.stack(sources, 0)
        slots = [
            lax.dynamic_index_in_dim(pool, jnp.bitwise_xor(mine, v), 0, keepdims=False)
            for v in range(size)
        ]
        held = jnp.stack(slots, done)
        held = held.reshape(held.shape[:done] + (2,) * len(step) + held.shape[done + 1 :])
        order = order + step[::-1]
        done += len(step)
    rank = sorted(range(done), key=lambda j: -order[j])
    held = held.transpose(rank + list(range(done, held.ndim)))
    return held.reshape((length,) + piece.shape)


def summed_by_halving(blocks, axis, steps):
    length = lax.axis_size(axis)
    me = lax.axis_index(axis)
    bits = []
    stride = length // 2
    while stride >= 1:
        bits.append(stride)
        stride //= 2
    held = blocks
    for step in steps:
        size = 2 ** len(step)
        mine = digit_of(me, step)
        rest = [b for b in bits if b not in step]
        front = held.reshape((2,) * len(bits) + blocks.shape[1:]) if bits else held
        lead = [bits.index(b) for b in step[::-1]] + [bits.index(b) for b in rest]
        front = front.transpose(lead + list(range(len(bits), front.ndim)))
        front = front.reshape((size,) + (2 ** len(rest),) + blocks.shape[1:])
        total = lax.dynamic_index_in_dim(front, mine, 0, keepdims=False)
        for p in range(1, size):
            give = lax.dynamic_index_in_dim(front, jnp.bitwise_xor(mine, p), 0, keepdims=False)
            total = total + exchanged(give, axis, mask_of(p, step))
        held = total
        bits = rest
    return held[0]

def summed_apart(parts, shared, axis, steps):
    count, height, size = parts.shape
    shared_rows = shared.reshape(height, -1)
    stacked = jnp.concatenate(
        [parts, jnp.broadcast_to(shared_rows[None], (count,) + shared_rows.shape)], 2
    )
    mine = summed_by_halving(stacked, axis, steps)
    return mine[:, :size], mine[:, size:].reshape(-1)

def on_device(
    branch_in, cotangent, weight_a, weight_x, conv_weight, conv_bias, bias_a, bias_x, rate
):
    inputs = branch_in[0]
    upstream = cotangent[0].astype(jnp.float32)
    length = inputs.shape[0]
    taps = conv_weight.shape[0]
    rows, cols = weight_a.shape
    dp_size = lax.axis_size("dp")
    ctx_size = lax.axis_size("ctx")
    packed = jnp.concatenate(
        [conv_weight, conv_bias[None], bias_a[None], bias_x[None], rate[None]], 0
    )
    width = ctx_size * cols
    head_width = dp_size * rows
    joined = jnp.concatenate([weight_a, weight_x, packed], 0)
    by_ctx = gathered_by_doubling(joined, "ctx", bit_steps(ctx_size))
    by_ctx = by_ctx.transpose(1, 0, 2).reshape(joined.shape[0], width)
    params = by_ctx[2 * rows :]
    heads = by_ctx[: 2 * rows].reshape(2 * rows, -1, head_width).transpose(1, 0, 2)
    by_dp = gathered_by_doubling(heads, "dp", near_last(dp_size))
    head_count = heads.shape[0]

    def head_major(part):
        return part.transpose(1, 0, 2, 3).reshape(head_count, dp_size * rows, head_width)

    full_a = head_major(by_dp[:, :, :rows])
    full_x = head_major(by_dp[:, :, rows:])
    params = params.astype(jnp.float32)
    taps_f = params[:taps]
    cbias = params[taps]
    abias = params[taps + 1]
    xbias = params[taps + 2]
    rates = params[taps + 3]
    tail = passed_along(inputs[length - (taps - 1) :], "ctx", 1)
    padded = jnp.concatenate([tail, inputs], 0).astype(jnp.float32)
    conv = cbias
    for tap in range(taps):
        conv = conv + taps_f[tap] * padded[tap : tap + length]
    conv_b = conv.astype(jnp.bfloat16)
    conv_f = conv_b.astype(jnp.float32)
    recur_gate = jax.nn.sigmoid(mix_heads(conv_b, full_a) + abias)
    input_gate = jax.nn.sigmoid(mix_heads(conv_b, full_x) + xbias)
    log_decay = -8.0 * recur_gate * rates
    decay = jnp.exp(log_decay)
    one_minus = -jnp.expm1(2.0 * log_decay)
    multiplier = jnp.sqrt(jnp.maximum(one_minus, floor_value))
    drive = multiplier * input_gate * conv_f

    row_id = lax.broadcasted_iota(jnp.int32, (length, length), 0)
    col_id = lax.broadcasted_iota(jnp.int32, (length, length), 1)
    lower = (row_id >= col_id).astype(jnp.float32)
    upper = (row_id <= col_id).astype(jnp.float32)
    cum_log = jnp.dot(lower, log_decay, precision=exact)
    grow = jnp.exp(cum_log)
    shrink = jnp.exp(-cum_log)
    local_hidden = grow * jnp.dot(lower, shrink * drive, precision=exact)
    weighted_back = jnp.dot(upper, grow * upstream, precision=exact)
    local_back = shrink * weighted_back
    block_decay = grow[-1]
    state_in, back_in = block_prefix(block_decay, local_hidden[-1], weighted_back[0], "ctx")
    hidden = local_hidden + grow * state_in
    previous = jnp.concatenate([state_in[None], hidden[:-1]], 0)
    back = local_back + (block_decay * shrink) * back_in
    slope = jnp.where(one_minus > floor_value, 0.5 / multiplier, 0.0)
    d_mult = back * input_gate * conv_f
    d_log = back * previous * decay - 2.0 * decay * decay * d_mult * slope
    d_recur = (d_log * (-8.0 * rates) * recur_gate * (1.0 - recur_gate)).astype(jnp.bfloat16)
    d_input = (back * multiplier * conv_f * input_gate * (1.0 - input_gate)).astype(jnp.bfloat16)
    d_conv = (
        back * multiplier * input_gate + back_heads(d_recur, full_a) + back_heads(d_input, full_x)
    )
    following = passed_along(d_conv[: taps - 1], "ctx", -1)
    dpad = jnp.concatenate([d_conv, following], 0)
    grad_in = jnp.zeros((length, width), jnp.float32)
    for tap in range(taps):
        start = taps - 1 - tap
        grad_in = grad_in + taps_f[tap] * dpad[start : start + length]
    local_wgrad = grad_heads(conv_b, d_recur, head_width)
    local_rgrad = jnp.sum(d_log * (-8.0 * recur_gate), axis=0)
    by_row = local_wgrad.reshape(dp_size, rows, width)
    row_sum, rgrad = summed_apart(by_row, local_rgrad, "dp", spread_steps(dp_size, 1))
    by_channel = row_sum.reshape(rows, ctx_size, cols).transpose(1, 0, 2)
    wgrad, rgrad = summed_apart(by_channel, rgrad, "ctx", digit_steps(ctx_size))
    return (grad_in.astype(jnp.bfloat16)[None], wgrad, rgrad)


def solution(mesh):
    placed = (
        P("dp", "ctx", None),
        P("dp", "ctx", None),
        P("dp", "ctx"),
        P("dp", "ctx"),
        P(None, "ctx"),
        P("ctx"),
        P("ctx"),
        P("ctx"),
        P("ctx"),
    )
    return jax.shard_map(
        on_device,
        mesh=mesh,
        in_specs=placed,
        out_specs=(P("dp", "ctx", None), P("dp", "ctx"), P()),
        check_vma=False,
    )
```

```python
import jax
import jax.numpy as jnp
from jax import lax
from jax.sharding import PartitionSpec as P

floor_value = 2.5e-07
exact = lax.Precision.HIGHEST


def passed_along(array, axis, by):
    length = lax.axis_size(axis)
    pairs = [(i, i + by) for i in range(length) if 0 <= i + by < length]
    return lax.ppermute(array, axis, pairs)


def mix_heads(values, weights):
    tokens = values.shape[0]
    head_count, head_width, _ = weights.shape
    left = values.reshape(tokens, head_count, head_width)
    result = jnp.einsum("thk,hkj->thj", left, weights, preferred_element_type=jnp.float32)
    return result.reshape(tokens, head_count * head_width)


def back_heads(grads, weights):
    tokens = grads.shape[0]
    head_count, head_width, _ = weights.shape
    left = grads.reshape(tokens, head_count, head_width)
    result = jnp.einsum("thj,hkj->thk", left, weights, preferred_element_type=jnp.float32)
    return result.reshape(tokens, head_count * head_width)


def grad_heads(values, grads, head_width):
    tokens = values.shape[0]
    head_count = values.shape[1] // head_width
    left = values.reshape(tokens, head_count, head_width)
    right = grads.reshape(tokens, head_count, head_width)
    result = jnp.einsum("thk,thj->khj", left, right, preferred_element_type=jnp.float32)
    return result.reshape(head_width, head_count * head_width)


def compose(own, received):
    return (own[0] * received[0], own[0] * received[1] + own[1])


def block_prefix(decay_all, forward_all, backward_all, axis):
    span = lax.axis_size(axis)
    me = lax.axis_index(axis)
    ones = jnp.ones_like(decay_all)
    zeros = jnp.zeros_like(decay_all)
    group = (decay_all, forward_all, backward_all)
    before = (ones, zeros)
    after = (ones, zeros)
    stride = 1
    while stride < span:
        got = exchanged(jnp.stack(group), axis, stride)
        other = (got[0], got[1], got[2])
        right_half = (me // stride) % 2 == 1
        mixed_before = compose(before, (other[0], other[1]))
        mixed_after = compose(after, (other[0], other[2]))
        before = tuple(jnp.where(right_half, n, o) for n, o in zip(mixed_before, before))
        after = tuple(jnp.where(right_half, o, n) for n, o in zip(mixed_after, after))
        forward_total = jnp.where(
            right_half, group[0] * other[1] + group[1], other[0] * group[1] + other[1]
        )
        backward_total = jnp.where(
            right_half, other[0] * group[2] + other[2], group[0] * other[2] + group[2]
        )
        group = (group[0] * other[0], forward_total, backward_total)
        stride *= 2
    return before[1], after[1]

def core_first_steps(length):
    bits = [stride for step in digit_steps(length) for stride in step]
    return [bits[:1]] + [bits[i : i + 2] for i in range(1, len(bits), 2)]


def spread_steps(length, first):
    bits = [stride for step in digit_steps(length) for stride in step]
    head, rest = bits[:first], bits[first:]
    half = (len(rest) + 1) // 2
    low, high = rest[:half], rest[half:]
    steps = [[b] for b in head]
    for i, b in enumerate(low):
        steps.append([b, high[i]] if i < len(high) else [b])
    return steps


def near_last(length):
    single = [[b] for b in [stride for step in spread_steps(length, 1) for stride in step]]
    return single[::-1]


def high_first(length):
    single = bit_steps(length)
    half = len(single) // 2
    return single[half:] + single[:half]


def bit_steps(length):
    return [[stride] for step in digit_steps(length) for stride in step]


def digit_steps(length):
    bits = []
    stride = 1
    while stride < length:
        bits.append(stride)
        stride *= 2
    return [bits[i : i + 2] for i in range(0, len(bits), 2)]


def exchanged(array, axis, mask):
    length = lax.axis_size(axis)
    return lax.ppermute(array, axis, [(i, i ^ mask) for i in range(length)])


def patterns(step):
    masks = [0]
    for stride in step:
        masks = masks + [m + stride for m in masks]
    return masks


def digit_of(me, step):
    value = jnp.int32(0)
    for place, stride in enumerate(step):
        value = value + ((me // stride) % 2) * (2**place)
    return value


def mask_of(pattern_index, step):
    mask = 0
    for place, stride in enumerate(step):
        if (pattern_index >> place) & 1:
            mask += stride
    return mask


def gathered_by_doubling(piece, axis, steps):
    length = lax.axis_size(axis)
    me = lax.axis_index(axis)
    held = piece
    done = 0
    order = []
    for step in steps:
        size = 2 ** len(step)
        mine = digit_of(me, step)
        sources = [held] + [exchanged(held, axis, mask_of(p, step)) for p in range(1, size)]
        pool = jnp.stack(sources, 0)
        slots = [
            lax.dynamic_index_in_dim(pool, jnp.bitwise_xor(mine, v), 0, keepdims=False)
            for v in range(size)
        ]
        held = jnp.stack(slots, done)
        held = held.reshape(held.shape[:done] + (2,) * len(step) + held.shape[done + 1 :])
        order = order + step[::-1]
        done += len(step)
    rank = sorted(range(done), key=lambda j: -order[j])
    held = held.transpose(rank + list(range(done, held.ndim)))
    return held.reshape((length,) + piece.shape)


def summed_by_halving(blocks, axis, steps):
    length = lax.axis_size(axis)
    me = lax.axis_index(axis)
    bits = []
    stride = length // 2
    while stride >= 1:
        bits.append(stride)
        stride //= 2
    held = blocks
    for step in steps:
        size = 2 ** len(step)
        mine = digit_of(me, step)
        rest = [b for b in bits if b not in step]
        front = held.reshape((2,) * len(bits) + blocks.shape[1:]) if bits else held
        lead = [bits.index(b) for b in step[::-1]] + [bits.index(b) for b in rest]
        front = front.transpose(lead + list(range(len(bits), front.ndim)))
        front = front.reshape((size,) + (2 ** len(rest),) + blocks.shape[1:])
        total = lax.dynamic_index_in_dim(front, mine, 0, keepdims=False)
        for p in range(1, size):
            give = lax.dynamic_index_in_dim(front, jnp.bitwise_xor(mine, p), 0, keepdims=False)
            total = total + exchanged(give, axis, mask_of(p, step))
        held = total
        bits = rest
    return held[0]

def summed_apart(parts, shared, axis, steps):
    count, height, size = parts.shape
    shared_rows = shared.reshape(height, -1)
    stacked = jnp.concatenate(
        [parts, jnp.broadcast_to(shared_rows[None], (count,) + shared_rows.shape)], 2
    )
    mine = summed_by_halving(stacked, axis, steps)
    return mine[:, :size], mine[:, size:].reshape(-1)

def on_device(
    branch_in, cotangent, weight_a, weight_x, conv_weight, conv_bias, bias_a, bias_x, rate
):
    inputs = branch_in[0]
    upstream = cotangent[0].astype(jnp.float32)
    length = inputs.shape[0]
    taps = conv_weight.shape[0]
    rows, cols = weight_a.shape
    dp_size = lax.axis_size("dp")
    ctx_size = lax.axis_size("ctx")
    packed = jnp.concatenate(
        [conv_weight, conv_bias[None], bias_a[None], bias_x[None], rate[None]], 0
    )
    width = ctx_size * cols
    head_width = dp_size * rows
    joined = jnp.concatenate([weight_a, weight_x, packed], 0)
    by_ctx = gathered_by_doubling(joined, "ctx", high_first(ctx_size))
    by_ctx = by_ctx.transpose(1, 0, 2).reshape(joined.shape[0], width)
    params = by_ctx[2 * rows :]
    heads = by_ctx[: 2 * rows].reshape(2 * rows, -1, head_width).transpose(1, 0, 2)
    by_dp = gathered_by_doubling(heads, "dp", near_last(dp_size))
    head_count = heads.shape[0]

    def head_major(part):
        return part.transpose(1, 0, 2, 3).reshape(head_count, dp_size * rows, head_width)

    full_a = head_major(by_dp[:, :, :rows])
    full_x = head_major(by_dp[:, :, rows:])
    params = params.astype(jnp.float32)
    taps_f = params[:taps]
    cbias = params[taps]
    abias = params[taps + 1]
    xbias = params[taps + 2]
    rates = params[taps + 3]
    tail = passed_along(inputs[length - (taps - 1) :], "ctx", 1)
    padded = jnp.concatenate([tail, inputs], 0).astype(jnp.float32)
    conv = cbias
    for tap in range(taps):
        conv = conv + taps_f[tap] * padded[tap : tap + length]
    conv_b = conv.astype(jnp.bfloat16)
    conv_f = conv_b.astype(jnp.float32)
    recur_gate = jax.nn.sigmoid(mix_heads(conv_b, full_a) + abias)
    input_gate = jax.nn.sigmoid(mix_heads(conv_b, full_x) + xbias)
    log_decay = -8.0 * recur_gate * rates
    decay = jnp.exp(log_decay)
    one_minus = -jnp.expm1(2.0 * log_decay)
    multiplier = jnp.sqrt(jnp.maximum(one_minus, floor_value))
    drive = multiplier * input_gate * conv_f

    row_id = lax.broadcasted_iota(jnp.int32, (length, length), 0)
    col_id = lax.broadcasted_iota(jnp.int32, (length, length), 1)
    lower = (row_id >= col_id).astype(jnp.float32)
    upper = (row_id <= col_id).astype(jnp.float32)
    cum_log = jnp.dot(lower, log_decay, precision=exact)
    grow = jnp.exp(cum_log)
    shrink = jnp.exp(-cum_log)
    local_hidden = grow * jnp.dot(lower, shrink * drive, precision=exact)
    weighted_back = jnp.dot(upper, grow * upstream, precision=exact)
    local_back = shrink * weighted_back
    block_decay = grow[-1]
    state_in, back_in = block_prefix(block_decay, local_hidden[-1], weighted_back[0], "ctx")
    hidden = local_hidden + grow * state_in
    previous = jnp.concatenate([state_in[None], hidden[:-1]], 0)
    back = local_back + (block_decay * shrink) * back_in
    slope = jnp.where(one_minus > floor_value, 0.5 / multiplier, 0.0)
    d_mult = back * input_gate * conv_f
    d_log = back * previous * decay - 2.0 * decay * decay * d_mult * slope
    d_recur = (d_log * (-8.0 * rates) * recur_gate * (1.0 - recur_gate)).astype(jnp.bfloat16)
    d_input = (back * multiplier * conv_f * input_gate * (1.0 - input_gate)).astype(jnp.bfloat16)
    d_conv = (
        back * multiplier * input_gate + back_heads(d_recur, full_a) + back_heads(d_input, full_x)
    )
    following = passed_along(d_conv[: taps - 1], "ctx", -1)
    dpad = jnp.concatenate([d_conv, following], 0)
    grad_in = jnp.zeros((length, width), jnp.float32)
    for tap in range(taps):
        start = taps - 1 - tap
        grad_in = grad_in + taps_f[tap] * dpad[start : start + length]
    local_wgrad = grad_heads(conv_b, d_recur, head_width)
    local_rgrad = jnp.sum(d_log * (-8.0 * recur_gate), axis=0)
    by_row = local_wgrad.reshape(dp_size, rows, width)
    row_sum, rgrad = summed_apart(by_row, local_rgrad, "dp", spread_steps(dp_size, 1))
    by_channel = row_sum.reshape(rows, ctx_size, cols).transpose(1, 0, 2)
    wgrad, rgrad = summed_apart(by_channel, rgrad, "ctx", digit_steps(ctx_size)[::-1])
    return (grad_in.astype(jnp.bfloat16)[None], wgrad, rgrad)


def solution(mesh):
    placed = (
        P("dp", "ctx", None),
        P("dp", "ctx", None),
        P("dp", "ctx"),
        P("dp", "ctx"),
        P(None, "ctx"),
        P("ctx"),
        P("ctx"),
        P("ctx"),
        P("ctx"),
    )
    return jax.shard_map(
        on_device,
        mesh=mesh,
        in_specs=placed,
        out_specs=(P("dp", "ctx", None), P("dp", "ctx"), P()),
        check_vma=False,
    )
```

```python
import jax
import jax.numpy as jnp
from jax import lax
from jax.sharding import PartitionSpec as P

floor_value = 2.5e-07
exact = lax.Precision.HIGHEST


def passed_along(array, axis, by):
    length = lax.axis_size(axis)
    pairs = [(i, i + by) for i in range(length) if 0 <= i + by < length]
    return lax.ppermute(array, axis, pairs)


def mix_heads(values, weights):
    tokens = values.shape[0]
    head_count, head_width, _ = weights.shape
    left = values.reshape(tokens, head_count, head_width)
    result = jnp.einsum("thk,hkj->thj", left, weights, preferred_element_type=jnp.float32)
    return result.reshape(tokens, head_count * head_width)


def back_heads(grads, weights):
    tokens = grads.shape[0]
    head_count, head_width, _ = weights.shape
    left = grads.reshape(tokens, head_count, head_width)
    result = jnp.einsum("thj,hkj->thk", left, weights, preferred_element_type=jnp.float32)
    return result.reshape(tokens, head_count * head_width)


def grad_heads(values, grads, head_width):
    tokens = values.shape[0]
    head_count = values.shape[1] // head_width
    left = values.reshape(tokens, head_count, head_width)
    right = grads.reshape(tokens, head_count, head_width)
    result = jnp.einsum("thk,thj->khj", left, right, preferred_element_type=jnp.float32)
    return result.reshape(head_width, head_count * head_width)


def compose(own, received):
    return (own[0] * received[0], own[0] * received[1] + own[1])


def block_prefix(decay_all, forward_all, backward_all, axis):
    span = lax.axis_size(axis)
    me = lax.axis_index(axis)
    ones = jnp.ones_like(decay_all)
    zeros = jnp.zeros_like(decay_all)
    group = (decay_all, forward_all, backward_all)
    before = (ones, zeros)
    after = (ones, zeros)
    stride = 1
    while stride < span:
        got = exchanged(jnp.stack(group), axis, stride)
        other = (got[0], got[1], got[2])
        right_half = (me // stride) % 2 == 1
        mixed_before = compose(before, (other[0], other[1]))
        mixed_after = compose(after, (other[0], other[2]))
        before = tuple(jnp.where(right_half, n, o) for n, o in zip(mixed_before, before))
        after = tuple(jnp.where(right_half, o, n) for n, o in zip(mixed_after, after))
        forward_total = jnp.where(
            right_half, group[0] * other[1] + group[1], other[0] * group[1] + other[1]
        )
        backward_total = jnp.where(
            right_half, other[0] * group[2] + other[2], group[0] * other[2] + group[2]
        )
        group = (group[0] * other[0], forward_total, backward_total)
        stride *= 2
    return before[1], after[1]

def core_first_steps(length):
    bits = [stride for step in digit_steps(length) for stride in step]
    return [bits[:1]] + [bits[i : i + 2] for i in range(1, len(bits), 2)]


def spread_steps(length, first):
    bits = [stride for step in digit_steps(length) for stride in step]
    head, rest = bits[:first], bits[first:]
    half = (len(rest) + 1) // 2
    low, high = rest[:half], rest[half:]
    steps = [[b] for b in head]
    for i, b in enumerate(low):
        steps.append([b, high[i]] if i < len(high) else [b])
    return steps


def near_last(length):
    single = [[b] for b in [stride for step in spread_steps(length, 1) for stride in step]]
    return single[::-1]


def bit_steps(length):
    return [[stride] for step in digit_steps(length) for stride in step]


def digit_steps(length):
    bits = []
    stride = 1
    while stride < length:
        bits.append(stride)
        stride *= 2
    return [bits[i : i + 2] for i in range(0, len(bits), 2)]


def exchanged(array, axis, mask):
    length = lax.axis_size(axis)
    return lax.ppermute(array, axis, [(i, i ^ mask) for i in range(length)])


def patterns(step):
    masks = [0]
    for stride in step:
        masks = masks + [m + stride for m in masks]
    return masks


def digit_of(me, step):
    value = jnp.int32(0)
    for place, stride in enumerate(step):
        value = value + ((me // stride) % 2) * (2**place)
    return value


def mask_of(pattern_index, step):
    mask = 0
    for place, stride in enumerate(step):
        if (pattern_index >> place) & 1:
            mask += stride
    return mask


def gathered_by_doubling(piece, axis, steps):
    length = lax.axis_size(axis)
    me = lax.axis_index(axis)
    held = piece
    done = 0
    order = []
    for step in steps:
        size = 2 ** len(step)
        mine = digit_of(me, step)
        sources = [held] + [exchanged(held, axis, mask_of(p, step)) for p in range(1, size)]
        pool = jnp.stack(sources, 0)
        slots = [
            lax.dynamic_index_in_dim(pool, jnp.bitwise_xor(mine, v), 0, keepdims=False)
            for v in range(size)
        ]
        held = jnp.stack(slots, done)
        held = held.reshape(held.shape[:done] + (2,) * len(step) + held.shape[done + 1 :])
        order = order + step[::-1]
        done += len(step)
    rank = sorted(range(done), key=lambda j: -order[j])
    held = held.transpose(rank + list(range(done, held.ndim)))
    return held.reshape((length,) + piece.shape)


def summed_by_halving(blocks, axis, steps):
    length = lax.axis_size(axis)
    me = lax.axis_index(axis)
    bits = []
    stride = length // 2
    while stride >= 1:
        bits.append(stride)
        stride //= 2
    held = blocks
    for step in steps:
        size = 2 ** len(step)
        mine = digit_of(me, step)
        rest = [b for b in bits if b not in step]
        front = held.reshape((2,) * len(bits) + blocks.shape[1:]) if bits else held
        lead = [bits.index(b) for b in step[::-1]] + [bits.index(b) for b in rest]
        front = front.transpose(lead + list(range(len(bits), front.ndim)))
        front = front.reshape((size,) + (2 ** len(rest),) + blocks.shape[1:])
        total = lax.dynamic_index_in_dim(front, mine, 0, keepdims=False)
        for p in range(1, size):
            give = lax.dynamic_index_in_dim(front, jnp.bitwise_xor(mine, p), 0, keepdims=False)
            total = total + exchanged(give, axis, mask_of(p, step))
        held = total
        bits = rest
    return held[0]

def summed_apart(parts, shared, axis, steps):
    count, height, size = parts.shape
    shared_rows = shared.reshape(height, -1)
    stacked = jnp.concatenate(
        [parts, jnp.broadcast_to(shared_rows[None], (count,) + shared_rows.shape)], 2
    )
    mine = summed_by_halving(stacked, axis, steps)
    return mine[:, :size], mine[:, size:].reshape(-1)

def on_device(
    branch_in, cotangent, weight_a, weight_x, conv_weight, conv_bias, bias_a, bias_x, rate
):
    inputs = branch_in[0]
    upstream = cotangent[0].astype(jnp.float32)
    length = inputs.shape[0]
    taps = conv_weight.shape[0]
    rows, cols = weight_a.shape
    dp_size = lax.axis_size("dp")
    ctx_size = lax.axis_size("ctx")
    packed = jnp.concatenate(
        [conv_weight, conv_bias[None], bias_a[None], bias_x[None], rate[None]], 0
    )
    width = ctx_size * cols
    head_width = dp_size * rows
    joined = jnp.concatenate([weight_a, weight_x, packed], 0)
    by_ctx = gathered_by_doubling(joined, "ctx", bit_steps(ctx_size))
    by_ctx = by_ctx.transpose(1, 0, 2).reshape(joined.shape[0], width)
    params = by_ctx[2 * rows :]
    heads = by_ctx[: 2 * rows].reshape(2 * rows, -1, head_width).transpose(1, 0, 2)
    by_dp = gathered_by_doubling(heads, "dp", near_last(dp_size))
    head_count = heads.shape[0]

    def head_major(part):
        return part.transpose(1, 0, 2, 3).reshape(head_count, dp_size * rows, head_width)

    full_a = head_major(by_dp[:, :, :rows])
    full_x = head_major(by_dp[:, :, rows:])
    params = params.astype(jnp.float32)
    taps_f = params[:taps]
    cbias = params[taps]
    abias = params[taps + 1]
    xbias = params[taps + 2]
    rates = params[taps + 3]
    tail = passed_along(inputs[length - (taps - 1) :], "ctx", 1)
    padded = jnp.concatenate([tail, inputs], 0).astype(jnp.float32)
    conv = cbias
    for tap in range(taps):
        conv = conv + taps_f[tap] * padded[tap : tap + length]
    conv_b = conv.astype(jnp.bfloat16)
    conv_f = conv_b.astype(jnp.float32)
    recur_gate = jax.nn.sigmoid(mix_heads(conv_b, full_a) + abias)
    input_gate = jax.nn.sigmoid(mix_heads(conv_b, full_x) + xbias)
    log_decay = -8.0 * recur_gate * rates
    decay = jnp.exp(log_decay)
    one_minus = -jnp.expm1(2.0 * log_decay)
    multiplier = jnp.sqrt(jnp.maximum(one_minus, floor_value))
    drive = multiplier * input_gate * conv_f

    row_id = lax.broadcasted_iota(jnp.int32, (length, length), 0)
    col_id = lax.broadcasted_iota(jnp.int32, (length, length), 1)
    lower = (row_id >= col_id).astype(jnp.float32)
    upper = (row_id <= col_id).astype(jnp.float32)
    cum_log = jnp.dot(lower, log_decay, precision=exact)
    grow = jnp.exp(cum_log)
    shrink = jnp.exp(-cum_log)
    local_hidden = grow * jnp.dot(lower, shrink * drive, precision=exact)
    weighted_back = jnp.dot(upper, grow * upstream, precision=exact)
    local_back = shrink * weighted_back
    block_decay = grow[-1]
    state_in, back_in = block_prefix(block_decay, local_hidden[-1], weighted_back[0], "ctx")
    hidden = local_hidden + grow * state_in
    previous = jnp.concatenate([state_in[None], hidden[:-1]], 0)
    back = local_back + (block_decay * shrink) * back_in
    slope = jnp.where(one_minus > floor_value, 0.5 / multiplier, 0.0)
    d_mult = back * input_gate * conv_f
    d_log = back * previous * decay - 2.0 * decay * decay * d_mult * slope
    d_recur = (d_log * (-8.0 * rates) * recur_gate * (1.0 - recur_gate)).astype(jnp.bfloat16)
    d_input = (back * multiplier * conv_f * input_gate * (1.0 - input_gate)).astype(jnp.bfloat16)
    d_conv = (
        back * multiplier * input_gate + back_heads(d_recur, full_a) + back_heads(d_input, full_x)
    )
    following = passed_along(d_conv[: taps - 1], "ctx", -1)
    dpad = jnp.concatenate([d_conv, following], 0)
    grad_in = jnp.zeros((length, width), jnp.float32)
    for tap in range(taps):
        start = taps - 1 - tap
        grad_in = grad_in + taps_f[tap] * dpad[start : start + length]
    local_wgrad = grad_heads(conv_b, d_recur, head_width)
    token_ones = jnp.ones((1, length), jnp.float32)
    local_rgrad = jnp.dot(token_ones, d_log * (-8.0 * recur_gate), precision=exact)[0]
    by_row = local_wgrad.reshape(dp_size, rows, width)
    row_sum, rgrad = summed_apart(by_row, local_rgrad, "dp", spread_steps(dp_size, 1))
    by_channel = row_sum.reshape(rows, ctx_size, cols).transpose(1, 0, 2)
    wgrad, rgrad = summed_apart(by_channel, rgrad, "ctx", digit_steps(ctx_size))
    return (grad_in.astype(jnp.bfloat16)[None], wgrad, rgrad)


def solution(mesh):
    placed = (
        P("dp", "ctx", None),
        P("dp", "ctx", None),
        P("dp", "ctx"),
        P("dp", "ctx"),
        P(None, "ctx"),
        P("ctx"),
        P("ctx"),
        P("ctx"),
        P("ctx"),
    )
    return jax.shard_map(
        on_device,
        mesh=mesh,
        in_specs=placed,
        out_specs=(P("dp", "ctx", None), P("dp", "ctx"), P()),
        check_vma=False,
    )
```

```python
import jax
import jax.numpy as jnp
from jax import lax
from jax.sharding import PartitionSpec as P

floor_value = 2.5e-07
exact = lax.Precision.HIGHEST


def passed_along(array, axis, by):
    length = lax.axis_size(axis)
    pairs = [(i, i + by) for i in range(length) if 0 <= i + by < length]
    return lax.ppermute(array, axis, pairs)


def mix_heads(values, weights):
    tokens = values.shape[0]
    head_count, head_width, _ = weights.shape
    left = values.reshape(tokens, head_count, head_width)
    result = jnp.einsum("thk,hkj->thj", left, weights, preferred_element_type=jnp.float32)
    return result.reshape(tokens, head_count * head_width)


def back_heads(grads, weights):
    tokens = grads.shape[0]
    head_count, head_width, _ = weights.shape
    left = grads.reshape(tokens, head_count, head_width)
    result = jnp.einsum("thj,hkj->thk", left, weights, preferred_element_type=jnp.float32)
    return result.reshape(tokens, head_count * head_width)


def grad_heads(values, grads, head_width):
    tokens = values.shape[0]
    head_count = values.shape[1] // head_width
    left = values.reshape(tokens, head_count, head_width)
    right = grads.reshape(tokens, head_count, head_width)
    result = jnp.einsum("thk,thj->khj", left, right, preferred_element_type=jnp.float32)
    return result.reshape(head_width, head_count * head_width)


def compose(own, received):
    return (own[0] * received[0], own[0] * received[1] + own[1])


def block_prefix(decay_all, forward_all, backward_all, axis):
    span = lax.axis_size(axis)
    me = lax.axis_index(axis)
    ones = jnp.ones_like(decay_all)
    zeros = jnp.zeros_like(decay_all)
    group = (decay_all, forward_all, backward_all)
    before = (ones, zeros)
    after = (ones, zeros)
    stride = 1
    while stride < span:
        got = exchanged(jnp.stack(group), axis, stride)
        other = (got[0], got[1], got[2])
        right_half = (me // stride) % 2 == 1
        mixed_before = compose(before, (other[0], other[1]))
        mixed_after = compose(after, (other[0], other[2]))
        before = tuple(jnp.where(right_half, n, o) for n, o in zip(mixed_before, before))
        after = tuple(jnp.where(right_half, o, n) for n, o in zip(mixed_after, after))
        forward_total = jnp.where(
            right_half, group[0] * other[1] + group[1], other[0] * group[1] + other[1]
        )
        backward_total = jnp.where(
            right_half, other[0] * group[2] + other[2], group[0] * other[2] + group[2]
        )
        group = (group[0] * other[0], forward_total, backward_total)
        stride *= 2
    return before[1], after[1]

def core_first_steps(length):
    bits = [stride for step in digit_steps(length) for stride in step]
    return [bits[:1]] + [bits[i : i + 2] for i in range(1, len(bits), 2)]


def spread_steps(length, first):
    bits = [stride for step in digit_steps(length) for stride in step]
    head, rest = bits[:first], bits[first:]
    half = (len(rest) + 1) // 2
    low, high = rest[:half], rest[half:]
    steps = [[b] for b in head]
    for i, b in enumerate(low):
        steps.append([b, high[i]] if i < len(high) else [b])
    return steps


def near_last(length):
    single = [[b] for b in [stride for step in spread_steps(length, 1) for stride in step]]
    return single[::-1]


def bit_steps(length):
    return [[stride] for step in digit_steps(length) for stride in step]


def digit_steps(length):
    bits = []
    stride = 1
    while stride < length:
        bits.append(stride)
        stride *= 2
    return [bits[i : i + 2] for i in range(0, len(bits), 2)]


def exchanged(array, axis, mask):
    length = lax.axis_size(axis)
    return lax.ppermute(array, axis, [(i, i ^ mask) for i in range(length)])


def patterns(step):
    masks = [0]
    for stride in step:
        masks = masks + [m + stride for m in masks]
    return masks


def digit_of(me, step):
    value = jnp.int32(0)
    for place, stride in enumerate(step):
        value = value + ((me // stride) % 2) * (2**place)
    return value


def mask_of(pattern_index, step):
    mask = 0
    for place, stride in enumerate(step):
        if (pattern_index >> place) & 1:
            mask += stride
    return mask


def gathered_by_doubling(piece, axis, steps):
    length = lax.axis_size(axis)
    me = lax.axis_index(axis)
    held = piece
    done = 0
    order = []
    for step in steps:
        size = 2 ** len(step)
        mine = digit_of(me, step)
        sources = [held] + [exchanged(held, axis, mask_of(p, step)) for p in range(1, size)]
        pool = jnp.stack(sources, 0)
        slots = [
            lax.dynamic_index_in_dim(pool, jnp.bitwise_xor(mine, v), 0, keepdims=False)
            for v in range(size)
        ]
        held = jnp.stack(slots, done)
        held = held.reshape(held.shape[:done] + (2,) * len(step) + held.shape[done + 1 :])
        order = order + step[::-1]
        done += len(step)
    rank = sorted(range(done), key=lambda j: -order[j])
    held = held.transpose(rank + list(range(done, held.ndim)))
    return held.reshape((length,) + piece.shape)


def summed_by_halving(blocks, axis, steps):
    length = lax.axis_size(axis)
    me = lax.axis_index(axis)
    bits = []
    stride = length // 2
    while stride >= 1:
        bits.append(stride)
        stride //= 2
    held = blocks
    for step in steps:
        size = 2 ** len(step)
        mine = digit_of(me, step)
        rest = [b for b in bits if b not in step]
        front = held.reshape((2,) * len(bits) + blocks.shape[1:]) if bits else held
        lead = [bits.index(b) for b in step[::-1]] + [bits.index(b) for b in rest]
        front = front.transpose(lead + list(range(len(bits), front.ndim)))
        front = front.reshape((size,) + (2 ** len(rest),) + blocks.shape[1:])
        total = lax.dynamic_index_in_dim(front, mine, 0, keepdims=False)
        for p in range(1, size):
            give = lax.dynamic_index_in_dim(front, jnp.bitwise_xor(mine, p), 0, keepdims=False)
            total = total + exchanged(give, axis, mask_of(p, step))
        held = total
        bits = rest
    return held[0]

def summed_apart(parts, shared, axis, steps):
    count, height, size = parts.shape
    shared_rows = shared.reshape(height, -1)
    stacked = jnp.concatenate(
        [parts, jnp.broadcast_to(shared_rows[None], (count,) + shared_rows.shape)], 2
    )
    mine = summed_by_halving(stacked, axis, steps)
    return mine[:, :size], mine[:, size:].reshape(-1)

def on_device(
    branch_in, cotangent, weight_a, weight_x, conv_weight, conv_bias, bias_a, bias_x, rate
):
    inputs = branch_in[0]
    upstream = cotangent[0].astype(jnp.float32)
    length = inputs.shape[0]
    taps = conv_weight.shape[0]
    rows, cols = weight_a.shape
    dp_size = lax.axis_size("dp")
    ctx_size = lax.axis_size("ctx")
    packed = jnp.concatenate(
        [conv_weight, conv_bias[None], bias_a[None], bias_x[None], rate[None]], 0
    )
    width = ctx_size * cols
    head_width = dp_size * rows
    joined = jnp.concatenate([weight_a, weight_x, packed], 0)
    by_ctx = gathered_by_doubling(joined, "ctx", bit_steps(ctx_size))
    by_ctx = by_ctx.transpose(1, 0, 2).reshape(joined.shape[0], width)
    params = by_ctx[2 * rows :]
    heads = by_ctx[: 2 * rows].reshape(2 * rows, -1, head_width).transpose(1, 0, 2)
    by_dp = gathered_by_doubling(heads, "dp", near_last(dp_size))
    head_count = heads.shape[0]

    def head_major(part):
        return part.transpose(1, 0, 2, 3).reshape(head_count, dp_size * rows, head_width)

    full_a = head_major(by_dp[:, :, :rows])
    full_x = head_major(by_dp[:, :, rows:])
    params = params.astype(jnp.float32)
    taps_f = params[:taps]
    cbias = params[taps]
    abias = params[taps + 1]
    xbias = params[taps + 2]
    rates = params[taps + 3]
    tail = passed_along(inputs[length - (taps - 1) :], "ctx", 1)
    padded = jnp.concatenate([tail, inputs], 0).astype(jnp.float32)
    conv = cbias
    for tap in range(taps):
        conv = conv + taps_f[tap] * padded[tap : tap + length]
    conv_b = conv.astype(jnp.bfloat16)
    conv_f = conv_b.astype(jnp.float32)
    recur_gate = jax.nn.sigmoid(mix_heads(conv_b, full_a) + abias)
    input_gate = jax.nn.sigmoid(mix_heads(conv_b, full_x) + xbias)
    log_decay = -8.0 * recur_gate * rates
    decay = jnp.exp(log_decay)
    one_minus = -jnp.expm1(2.0 * log_decay)
    multiplier = jnp.sqrt(jnp.maximum(one_minus, floor_value))
    drive = multiplier * input_gate * conv_f

    row_id = lax.broadcasted_iota(jnp.int32, (length, length), 0)
    col_id = lax.broadcasted_iota(jnp.int32, (length, length), 1)
    lower = (row_id >= col_id).astype(jnp.float32)
    upper = (row_id <= col_id).astype(jnp.float32)
    cum_log = jnp.dot(lower, log_decay, precision=exact)
    grow = jnp.exp(cum_log)
    shrink = jnp.exp(-cum_log)
    local_hidden = grow * jnp.dot(lower, shrink * drive, precision=exact)
    weighted_back = jnp.dot(upper, grow * upstream, precision=exact)
    local_back = shrink * weighted_back
    block_decay = grow[-1]
    state_in, back_in = block_prefix(block_decay, local_hidden[-1], weighted_back[0], "ctx")
    hidden = local_hidden + grow * state_in
    previous = jnp.concatenate([state_in[None], hidden[:-1]], 0)
    back = local_back + (block_decay * shrink) * back_in
    slope = jnp.where(one_minus > floor_value, 0.5 / multiplier, 0.0)
    d_mult = back * input_gate * conv_f
    d_log = back * previous * decay - 2.0 * decay * decay * d_mult * slope
    d_recur = (d_log * (-8.0 * rates) * recur_gate * (1.0 - recur_gate)).astype(jnp.bfloat16)
    d_input = (back * multiplier * conv_f * input_gate * (1.0 - input_gate)).astype(jnp.bfloat16)
    d_conv = (
        back * multiplier * input_gate + back_heads(d_recur, full_a) + back_heads(d_input, full_x)
    )
    following = passed_along(d_conv[: taps - 1], "ctx", -1)
    dpad = jnp.concatenate([d_conv, following], 0)
    grad_in = jnp.zeros((length, width), jnp.float32)
    for tap in range(taps):
        start = taps - 1 - tap
        grad_in = grad_in + taps_f[tap] * dpad[start : start + length]
    local_wgrad = grad_heads(conv_b, d_recur, head_width)
    local_rgrad = jnp.sum(d_log * (-8.0 * recur_gate), axis=0)
    by_row = local_wgrad.reshape(dp_size, rows, width)
    row_sum, rgrad = summed_apart(by_row, local_rgrad, "dp", spread_steps(dp_size, 1))
    by_channel = row_sum.reshape(rows, ctx_size, cols).transpose(1, 0, 2)
    wgrad, rgrad = summed_apart(by_channel, rgrad, "ctx", bit_steps(ctx_size))
    return (grad_in.astype(jnp.bfloat16)[None], wgrad, rgrad)


def solution(mesh):
    placed = (
        P("dp", "ctx", None),
        P("dp", "ctx", None),
        P("dp", "ctx"),
        P("dp", "ctx"),
        P(None, "ctx"),
        P("ctx"),
        P("ctx"),
        P("ctx"),
        P("ctx"),
    )
    return jax.shard_map(
        on_device,
        mesh=mesh,
        in_specs=placed,
        out_specs=(P("dp", "ctx", None), P("dp", "ctx"), P()),
        check_vma=False,
    )
```
